128 devices in a mesh: br: 8 (over y_lo, z), bus: 16 (over y_hi, x, core).
Axes of the slice: x: 4, y: 4 (y_hi: 2, y_lo: 2; y = y_hi * 2 + y_lo), z: 4, core: 2. Of those that a mesh axis runs over, the one named last changes fastest.
Arguments:
- shift_factors: bfloat16 [65536, 8192], P('br', 'bus'), may hold values from -0.09375 to 0.09375
- injections: float32 [8192, 384], P('bus'), may hold values from -6 to 6
- prices: float32 [65536, 384], P(('br', 'bus')), may hold values from -6 to 6
- limits: float32 [65536], P(('br', 'bus')), may hold values from 0.2 to 2
- unit_cost: float32 [8192], P('bus'), may hold values from -1 to 1
- bus_load: float32 [8192], P('bus'), may hold values from 0.5 to 3
- bus_capacity: float32 [8192], P('bus'), may hold values from 0.5 to 3
- irradiance_profile: float32 [64, 1024], replicated, may hold values from 0 to 1
- plant_group: int32 [8192], P('bus'), may hold values from 0 to 1023
- scenario_profile: int32 [384], replicated, may hold values from 0 to 63
- listed_slab: int32 [1024, 3], replicated, may hold values from 0 to 7, all different within a row; in each aligned block of 8 rows (0 to 7, 8 to 15, ...) at most 6 rows name the same one
- listed_block: int32 [1024, 3], replicated, may hold values from 0 to 15
- rent_weight: bfloat16 [1024, 1536], P(('br', 'bus')), may hold values from -0.15625 to 0.15625
Outputs:
- new_injections: float32 [8192, 384], P('bus')
- new_prices: float32 [65536, 384], P(('br', 'bus'))
- group_rent: float32 [1024, 384], P(('br', 'bus'))
The draws below stay inside these ranges and needn't reach their ends.
Inputs may be any that keep to these rules, and one draw needn't show every extreme that they name: `listed_slab`: each plant group names 3 different slabs; among the 8 plant groups of one device (aligned blocks of 8 rows) no slab is named by more than 6 groups, and some device's groups name one slab exactly 6 times.
All inputs are finite; a program needn't handle non-finite values.
Results may differ from the reference program's by a relative error of at most 0.0052.
Values may be sent and summed in bfloat16 or wider, within the bound.
No kernel may reach another device: no remote copies, remote signals or barrier semaphores. Data moves between devices by JAX's collectives and lax.ppermute only.
A program may use at most 128 MiB of HBM per device.

```python
import math
import jax
import jax.numpy as jnp
import numpy as np
from jax import lax

BRANCHES = 65536
BUSES = 8192
SCEN = 384
BLOCK = 512
LISTS = 3
CAP = 6
GDEV = 8
PROFILES = 64
SLAB = 8192
GROUPS = 1024
N_BR = 8


def set_ends(drawn, rng, least, high):
    longest = drawn.shape.index(max(drawn.shape))
    spots = []
    for shift in (0, 1):
        where = [jax.random.randint(jax.random.fold_in(rng, axis), (), 0, length) for axis, length in enumerate(drawn.shape)]
        where[longest] = (where[longest] + shift) % drawn.shape[longest]
        spots.append(tuple(where))
    return drawn.at[spots[0]].set(least).at[spots[1]].set(high)


def raised(drawn, rng, source, target, blocks, factor):
    def block_of(dim):
        return (jnp.arange(drawn.shape[dim]) // (drawn.shape[dim] // blocks)).reshape((-1,) + (1,) * (drawn.ndim - 1 - dim))

    near = jax.random.permutation(rng, blocks)[block_of(target)]
    far = (block_of(target) + blocks // 2) % blocks
    return jnp.where((block_of(source) == near) | (block_of(source) == far), factor * drawn, drawn)


def block_levels(key, extent, split, least, high):
    gain, own = 1.0, jax.random.fold_in(key, 6)
    for axis_at, parts in split:
        steps = jnp.exp(jax.random.uniform(jax.random.fold_in(own, axis_at), (parts,), jnp.float32, least / len(split), high / len(split)))
        gain = gain * jnp.repeat(steps, extent[axis_at] // parts).reshape([-1 if axis == axis_at else 1 for axis in range(len(extent))])
    return gain


def assign_block(key, own, number, rows, number_of, top, most, skew):
    order = jax.random.permutation(key, number_of)
    packed, ordinary = shares(number_of, rows * top, most, skew, True), shares(number_of, rows * top, most, skew, False)
    places = jnp.arange(number_of)

    def named(tallies, turn):
        used = int((tallies > 0).sum())
        fixed = max(1, used // 4)
        shifted = fixed + (places - fixed + turn * (used - fixed)) % max(1, number_of - fixed)
        return jnp.zeros((number_of,), jnp.int32).at[order[jnp.where(places < fixed, places, shifted)]].set(jnp.asarray(tallies, jnp.int32))

    tallies = jnp.where(number % 4 == 0, named(packed, number // 4), named(ordinary, number - number // 4 - 1))
    mixed = jax.random.permutation(jax.random.fold_in(own, 3), number_of)
    donor, receiver = mixed[0:number_of // 2 * 2:2], mixed[1:number_of // 2 * 2:2]
    room = jnp.minimum(tallies[donor] - 1, most - tallies[receiver]) // 2
    room = jnp.where((donor == order[0]) | (receiver == order[0]) | (tallies[receiver] == 0), 0, jnp.maximum(room, 0))
    shifted = jax.random.randint(jax.random.fold_in(own, 4), (number_of // 2,), 0, 1 << 20) % (room + 1)
    tallies = tallies.at[donor].add(-shifted).at[receiver].add(shifted)
    labels = jnp.searchsorted(jnp.cumsum(tallies), jnp.arange(rows * top), side="right").astype(jnp.int32)
    listing = labels.reshape(top, rows).T
    listing = listing[jax.random.permutation(jax.random.fold_in(own, 1), rows)]
    turn = jax.random.randint(jax.random.fold_in(own, 2), (rows, 1), 0, top)
    return jnp.take_along_axis(listing, (jnp.arange(top)[None, :] + turn) % top, axis=1)


def shares(count, total, most, slope, full):
    weights = [(1 << 20) // math.isqrt(grade ** slope) + 1 for grade in range(1, count + 1)]
    largest = most if full else min(most, max(-(-total // count), total * weights[0] // sum(weights)))
    least = 1 if total - largest >= count - 1 else 0
    holding, surplus = [largest] + [least] * (count - 1), total - largest - least * (count - 1)
    while surplus > 0:
        candidates = [i for i in range(1, count) if holding[i] < largest] or [i for i in range(1, count) if holding[i] < most]
        pool, left = sum([weights[i] for i in candidates]), surplus
        for i in candidates:
            more = min(most - holding[i], max(1, left * weights[i] // pool), surplus)
            holding[i] = holding[i] + more
            surplus = surplus - more
    return np.array(holding)


def gaussian(stream_key, dims, scale, reach, pieces=(), held_as=jnp.bfloat16):
    level = block_levels(stream_key, dims, pieces, -0.22, 0.18) if pieces else 1.0
    result = jax.random.normal(stream_key, dims, jnp.float32) * scale * level
    return jnp.minimum(jnp.maximum(result, -reach), reach).astype(held_as)


def bell_draw_with(own_key, extent, width, most, split, heavy, dtype=jnp.bfloat16):
    array = width * jax.random.normal(own_key, extent, jnp.float32)
    if split:
        array = array * block_levels(own_key, extent, split, -0.22, 0.18)
    return jnp.clip(raised(array, jax.random.fold_in(own_key, 3), *heavy), -most, most).astype(dtype)


def setup_inputs(seed: int = 0) -> dict:
    streams_of = jax.random.split(jax.random.key(seed), 14)
    shift_factors = bell_draw_with(streams_of[0], (BRANCHES, BUSES), BUSES ** -0.5, 0.09375, ((0, 8), (1, 16)), (1, 0, 16, 2.0))
    injections = gaussian(streams_of[1], (BUSES, SCEN), 1.0, 6.0, ((0, 16),), jnp.float32)
    prices = gaussian(streams_of[2], (BRANCHES, SCEN), 1.0, 6.0, ((0, 128),), jnp.float32)
    limits = jnp.clip(jnp.exp(math.log(2.0) - 2.3025851 * jax.random.uniform(streams_of[3], (BRANCHES,), jnp.float32) ** block_levels(streams_of[3], (BRANCHES,), ((0, 128),), -0.2, 0.2)), 0.2, 2.0)
    unit_cost = jnp.clip(jax.random.uniform(streams_of[4], (BUSES,), jnp.float32, -1.0, 1.0) * block_levels(streams_of[4], (BUSES,), ((0, 16),), -0.4, 0.0), -1.0, 1.0)
    bus_load = jnp.clip(jnp.exp(math.log(3.0) - 1.7917595 * jax.random.uniform(streams_of[5], (BUSES,), jnp.float32) ** block_levels(streams_of[5], (BUSES,), ((0, 16),), -0.2, 0.2)), 0.5, 3.0)
    bus_capacity = jnp.clip(jnp.exp(math.log(3.0) - 1.7917595 * jax.random.uniform(streams_of[6], (BUSES,), jnp.float32) ** block_levels(streams_of[6], (BUSES,), ((0, 16),), -0.2, 0.2)), 0.5, 3.0)
    irradiance_profile = jnp.clip(jax.random.uniform(streams_of[7], (PROFILES, GROUPS), jnp.float32, 0.0, 1.0), 0.0, 1.0)
    plant_group = set_ends(jax.random.randint(streams_of[8], (BUSES,), 0, GROUPS), jax.random.fold_in(streams_of[8], 1), 0, GROUPS - 1).astype(jnp.int32)
    scenario_profile = set_ends(jax.random.randint(streams_of[9], (SCEN,), 0, PROFILES), jax.random.fold_in(streams_of[9], 1), 0, PROFILES - 1).astype(jnp.int32)
    listed_slab_keys = jax.random.split(jax.random.fold_in(streams_of[10], 1), GROUPS // GDEV)
    listed_slab_turns = jax.random.permutation(jax.random.fold_in(streams_of[10], 3), GROUPS // GDEV)
    listed_slab = jax.vmap(lambda own, number: assign_block(jax.random.fold_in(streams_of[10], 2), own, number, GDEV, N_BR, LISTS, CAP, 2))(listed_slab_keys, listed_slab_turns).reshape((GROUPS, LISTS))
    listed_block = set_ends(jax.random.randint(streams_of[11], (GROUPS, LISTS), 0, SLAB // BLOCK), jax.random.fold_in(streams_of[11], 1), 0, (SLAB // BLOCK) - 1).astype(jnp.int32)
    rent_weight = gaussian(streams_of[12], (GROUPS, LISTS * BLOCK), (LISTS * BLOCK) ** -0.5, 0.15625, ((0, 128),))
    return dict(shift_factors=shift_factors, injections=injections, prices=prices, limits=limits, unit_cost=unit_cost, bus_load=bus_load, bus_capacity=bus_capacity, irradiance_profile=irradiance_profile, plant_group=plant_group, scenario_profile=scenario_profile, listed_slab=listed_slab, listed_block=listed_block, rent_weight=rent_weight)


step_dual = 0.5
step_primal = 0.25


def reference(shift_factors, injections, prices, limits, unit_cost, bus_load, bus_capacity, irradiance_profile, plant_group, scenario_profile, listed_slab, listed_block, rent_weight):
    inject_half = injections.astype(jnp.bfloat16)
    flow = jnp.dot(shift_factors, inject_half, preferred_element_type=jnp.float32)
    moved = prices + step_dual * flow
    bound = step_dual * limits[:, None]
    new_prices = moved - jnp.clip(moved, -bound, bound)
    price_half = new_prices.astype(jnp.bfloat16)
    gradient = jnp.dot(shift_factors.T, price_half, preferred_element_type=jnp.float32)
    share = irradiance_profile[scenario_profile][:, plant_group].T
    upper = bus_capacity[:, None] * share
    trial = injections - step_primal * (unit_cost[:, None] + gradient)
    new_injections = jnp.minimum(jnp.maximum(trial, -bus_load[:, None]), upper)
    blocks = price_half.reshape(BRANCHES // BLOCK, BLOCK, SCEN)
    block_ids = (listed_slab * (SLAB // BLOCK) + listed_block).astype(jnp.int32)
    weights = rent_weight.reshape(GROUPS, LISTS, BLOCK)

    def one_group(item):
        weight_rows, ids = item
        picked = jnp.take(blocks, ids, axis=0).astype(jnp.float32)
        return jnp.einsum("kr,krs->s", weight_rows.astype(jnp.float32), picked)

    group_rent = lax.map(one_group, (weights, block_ids))
    return new_injections, new_prices, group_rent
```

```python
import jax
import jax.numpy as jnp
from jax import lax
from jax.sharding import PartitionSpec as P

BLOCK = 512
CAP = 6
GDEV = 8


step_dual = 0.5
step_primal = 0.25


def slots_of(slabs):
    positions = jnp.arange(slabs.shape[-1], dtype=jnp.int32)
    earlier = positions[None, :] < positions[:, None]
    same = slabs[..., :, None] == slabs[..., None, :]
    return jnp.sum((same & earlier).astype(jnp.int32), axis=-1)


def per_device(
    shift_factors,
    injections,
    prices,
    limits,
    unit_cost,
    bus_load,
    bus_capacity,
    irradiance_profile,
    plant_group,
    scenario_profile,
    listed_slab,
    listed_block,
    rent_weight,
):
    scenarios = injections.shape[1]
    bus_axis = lax.axis_size("bus")
    slab_axis = lax.axis_size("br")
    slab_index = lax.axis_index("br")
    column_index = lax.axis_index("bus")
    list_len = listed_slab.shape[1]
    entries = GDEV * list_len
    slab_rows = shift_factors.shape[0]
    blocks_per_slab = slab_rows // BLOCK

    slab_by_device = listed_slab.reshape(-1, entries)
    block_by_device = listed_block.reshape(-1, entries)
    self_device = slab_index * bus_axis + column_index
    own_slab = lax.dynamic_index_in_dim(slab_by_device, self_device, 0, keepdims=False)
    own_slot = slots_of(own_slab)
    slab_range = jnp.arange(slab_axis, dtype=jnp.int32)
    slot_range = jnp.arange(CAP, dtype=jnp.int32)
    pick_out = (own_slab[None, None, :] == slab_range[:, None, None]) & (
        own_slot[None, None, :] == slot_range[None, :, None]
    )
    weight_rows = rent_weight.reshape(entries, BLOCK)
    outgoing_w = jnp.einsum(
        "sce,er->scr", pick_out.astype(jnp.bfloat16), weight_rows, preferred_element_type=jnp.float32
    ).astype(jnp.bfloat16)
    arrived_w = lax.all_to_all(outgoing_w, "br", 0, 0, tiled=True)

    inject_half = injections.astype(jnp.bfloat16)
    flow = lax.psum_scatter(
        jnp.dot(shift_factors, inject_half, preferred_element_type=jnp.float32),
        "bus",
        scatter_dimension=0,
        tiled=True,
    )
    moved = prices + step_dual * flow
    bound = step_dual * limits[:, None]
    new_prices = moved - jnp.clip(moved, -bound, bound)
    price_half = new_prices.astype(jnp.bfloat16)
    slab_prices = lax.all_gather(price_half, "bus", axis=0, tiled=True)
    partial_grad = lax.dot_general(
        shift_factors, slab_prices, (((0,), (0,)), ((), ())), preferred_element_type=jnp.float32
    )

    bus_rows = partial_grad.shape[0]
    share_rows = bus_rows // slab_axis
    gathered = lax.all_to_all(partial_grad.reshape(slab_axis, share_rows, scenarios), "br", 0, 0, tiled=True)
    gradient = jnp.sum(gathered, axis=0)
    start = slab_index * share_rows
    my_inj = lax.dynamic_slice_in_dim(injections, start, share_rows, 0)
    my_cost = lax.dynamic_slice_in_dim(unit_cost, start, share_rows, 0)
    my_load = lax.dynamic_slice_in_dim(bus_load, start, share_rows, 0)
    my_cap = lax.dynamic_slice_in_dim(bus_capacity, start, share_rows, 0)
    my_group = lax.dynamic_slice_in_dim(plant_group, start, share_rows, 0)
    by_group = jnp.take(irradiance_profile, my_group, axis=1)
    share = jnp.take(by_group, scenario_profile, axis=0).T
    upper = my_cap[:, None] * share
    trial = my_inj - step_primal * (my_cost[:, None] + gradient)
    my_new = jnp.minimum(jnp.maximum(trial, -my_load[:, None]), upper)
    new_injections = lax.all_to_all(
        jnp.broadcast_to(my_new[None], (slab_axis, share_rows, scenarios)), "br", 0, 0, tiled=True
    ).reshape(bus_rows, scenarios)

    sources = slab_range * bus_axis + column_index
    src_slab = jnp.take(slab_by_device, sources, axis=0)
    src_block = jnp.take(block_by_device, sources, axis=0)
    src_slot = slots_of(src_slab)
    pick_in = (src_slab[:, None, :] == slab_index) & (src_slot[:, None, :] == slot_range[None, :, None])
    block_choice = jnp.sum(jnp.where(pick_in, src_block[:, None, :], 0), axis=2)
    block_hot = block_choice[:, :, None] == jnp.arange(blocks_per_slab, dtype=jnp.int32)[None, None, :]
    masked = jnp.where(block_hot[:, :, :, None], arrived_w[:, :, None, :], jnp.zeros((), jnp.bfloat16))
    masked = masked.reshape(slab_axis * CAP, slab_rows)
    partial_rent = jnp.dot(masked, slab_prices, preferred_element_type=jnp.float32)
    returned = lax.all_to_all(partial_rent.reshape(slab_axis, CAP, scenarios), "br", 0, 0, tiled=True)
    lookup = own_slab * CAP + own_slot
    fetched = jnp.take(returned.reshape(slab_axis * CAP, scenarios), lookup, axis=0)
    group_rent = jnp.sum(fetched.reshape(GDEV, list_len, scenarios), axis=1)
    return (new_injections, new_prices, group_rent)


def solution(mesh):
    placed = (
        P("br", "bus"),
        P("bus", None),
        P(("br", "bus"), None),
        P(("br", "bus")),
        P("bus"),
        P("bus"),
        P("bus"),
        P(),
        P("bus"),
        P(),
        P(),
        P(),
        P(("br", "bus"), None),
    )
    return jax.shard_map(
        per_device,
        mesh=mesh,
        in_specs=placed,
        out_specs=(P("bus", None), P(("br", "bus"), None), P(("br", "bus"), None)),
        check_vma=False,
    )
```

```python
import jax
import jax.numpy as jnp
from jax import lax
from jax.sharding import PartitionSpec as P

BLOCK = 512
CAP = 6
GDEV = 8


step_dual = 0.5
step_primal = 0.25


YHI, XR, CORES = 2, 4, 2


def bus_place():
    b = lax.axis_index("bus")
    return b // (XR * CORES), (b // CORES) % XR, b % CORES


def bus_perm(move):
    pairs = []
    for b in range(YHI * XR * CORES):
        yh, xi, c = b // (XR * CORES), (b // CORES) % XR, b % CORES
        ty, tx, tc = move(yh, xi, c)
        pairs.append((b, (ty * XR + tx) * CORES + tc))
    return pairs


CORE_SWAP = bus_perm(lambda y, x, c: (y, x, 1 - c))
X_UP = bus_perm(lambda y, x, c: (y, (x + 1) % XR, c))
X_DOWN = bus_perm(lambda y, x, c: (y, (x - 1) % XR, c))
Y_SWAP = bus_perm(lambda y, x, c: (1 - y, x, c))


def pick(a, i, axis):
    return lax.dynamic_index_in_dim(a, i, axis, keepdims=False)


def ring_scatter(parts, xi, up):
    step = 1 if up else -1
    perm = X_UP if up else X_DOWN
    acc = pick(parts, (xi - step) % XR, 0)
    for k in range(XR - 1):
        acc = lax.ppermute(acc, "bus", perm) + pick(parts, (xi - step * (k + 2)) % XR, 0)
    return acc


def ring_gather(own, xi, up):
    step = 1 if up else -1
    perm = X_UP if up else X_DOWN
    got = [own]
    for _ in range(XR - 1):
        got.append(lax.ppermute(got[-1], "bus", perm))
    stacked = jnp.stack(got)
    order = (step * (xi - jnp.arange(XR, dtype=jnp.int32))) % XR
    return jnp.take(stacked, order, axis=0)


def bus_reduce_scatter(send, keep):
    yh, xi, c = bus_place()
    y = keep + lax.ppermute(send, "bus", CORE_SWAP)
    half = y.shape[2] // 2
    cw = ring_scatter(jnp.moveaxis(y[:, :, :half], 1, 0), xi, True)
    ccw = ring_scatter(jnp.moveaxis(y[:, :, half:], 1, 0), xi, False)
    z = jnp.concatenate([cw, ccw], axis=1)
    return pick(z, yh, 0) + lax.ppermute(pick(z, 1 - yh, 0), "bus", Y_SWAP)


def bus_all_gather(p):
    yh, xi, c = bus_place()
    other = lax.ppermute(p, "bus", Y_SWAP)
    pair = jnp.where(yh == 0, jnp.stack([p, other]), jnp.stack([other, p]))
    half = p.shape[0] // 2
    cw = ring_gather(pair[:, :half], xi, True)
    ccw = ring_gather(pair[:, half:], xi, False)
    quad = jnp.moveaxis(jnp.concatenate([cw, ccw], axis=2), 0, 1)
    mate = lax.ppermute(quad, "bus", CORE_SWAP)
    full = jnp.where(c == 0, jnp.stack([quad, mate], axis=2), jnp.stack([mate, quad], axis=2))
    return full.reshape(-1, p.shape[1])


def slots_of(slabs):
    positions = jnp.arange(slabs.shape[-1], dtype=jnp.int32)
    earlier = positions[None, :] < positions[:, None]
    same = slabs[..., :, None] == slabs[..., None, :]
    return jnp.sum((same & earlier).astype(jnp.int32), axis=-1)


def per_device(
    shift_factors,
    injections,
    prices,
    limits,
    unit_cost,
    bus_load,
    bus_capacity,
    irradiance_profile,
    plant_group,
    scenario_profile,
    listed_slab,
    listed_block,
    rent_weight,
):
    scenarios = injections.shape[1]
    bus_axis = lax.axis_size("bus")
    slab_axis = lax.axis_size("br")
    slab_index = lax.axis_index("br")
    column_index = lax.axis_index("bus")
    list_len = listed_slab.shape[1]
    entries = GDEV * list_len
    slab_rows = shift_factors.shape[0]
    blocks_per_slab = slab_rows // BLOCK

    slab_by_device = listed_slab.reshape(-1, entries)
    block_by_device = listed_block.reshape(-1, entries)
    self_device = slab_index * bus_axis + column_index
    own_slab = lax.dynamic_index_in_dim(slab_by_device, self_device, 0, keepdims=False)
    own_slot = slots_of(own_slab)
    slab_range = jnp.arange(slab_axis, dtype=jnp.int32)
    slot_range = jnp.arange(CAP, dtype=jnp.int32)
    pick_out = (own_slab[None, None, :] == slab_range[:, None, None]) & (
        own_slot[None, None, :] == slot_range[None, :, None]
    )
    weight_rows = rent_weight.reshape(entries, BLOCK)
    outgoing_w = jnp.einsum(
        "sce,er->scr", pick_out.astype(jnp.bfloat16), weight_rows, preferred_element_type=jnp.float32
    ).astype(jnp.bfloat16)
    arrived_w = lax.all_to_all(outgoing_w, "br", 0, 0, tiled=True)

    inject_half = injections.astype(jnp.bfloat16)
    yh, xi, core = bus_place()
    by_place = shift_factors.reshape(YHI, XR, CORES, -1, shift_factors.shape[1])
    flow_send = jnp.dot(pick(by_place, 1 - core, 2), inject_half, preferred_element_type=jnp.float32)
    flow_keep = jnp.dot(pick(by_place, core, 2), inject_half, preferred_element_type=jnp.float32)
    flow = bus_reduce_scatter(flow_send, flow_keep)
    moved = prices + step_dual * flow
    bound = step_dual * limits[:, None]
    new_prices = moved - jnp.clip(moved, -bound, bound)
    price_half = new_prices.astype(jnp.bfloat16)
    slab_prices = bus_all_gather(price_half)
    partial_grad = lax.dot_general(
        shift_factors, slab_prices, (((0,), (0,)), ((), ())), preferred_element_type=jnp.float32
    )

    bus_rows = partial_grad.shape[0]
    share_rows = bus_rows // slab_axis
    gathered = lax.all_to_all(partial_grad.reshape(slab_axis, share_rows, scenarios), "br", 0, 0, tiled=True)
    gradient = jnp.sum(gathered, axis=0)
    start = slab_index * share_rows
    my_inj = lax.dynamic_slice_in_dim(injections, start, share_rows, 0)
    my_cost = lax.dynamic_slice_in_dim(unit_cost, start, share_rows, 0)
    my_load = lax.dynamic_slice_in_dim(bus_load, start, share_rows, 0)
    my_cap = lax.dynamic_slice_in_dim(bus_capacity, start, share_rows, 0)
    my_group = lax.dynamic_slice_in_dim(plant_group, start, share_rows, 0)
    by_group = jnp.take(irradiance_profile, my_group, axis=1)
    share = jnp.take(by_group, scenario_profile, axis=0).T
    upper = my_cap[:, None] * share
    trial = my_inj - step_primal * (my_cost[:, None] + gradient)
    my_new = jnp.minimum(jnp.maximum(trial, -my_load[:, None]), upper)
    new_injections = lax.all_to_all(
        jnp.broadcast_to(my_new[None], (slab_axis, share_rows, scenarios)), "br", 0, 0, tiled=True
    ).reshape(bus_rows, scenarios)

    sources = slab_range * bus_axis + column_index
    src_slab = jnp.take(slab_by_device, sources, axis=0)
    src_block = jnp.take(block_by_device, sources, axis=0)
    src_slot = slots_of(src_slab)
    pick_in = (src_slab[:, None, :] == slab_index) & (src_slot[:, None, :] == slot_range[None, :, None])
    block_choice = jnp.sum(jnp.where(pick_in, src_block[:, None, :], 0), axis=2)
    block_hot = block_choice[:, :, None] == jnp.arange(blocks_per_slab, dtype=jnp.int32)[None, None, :]
    masked = jnp.where(block_hot[:, :, :, None], arrived_w[:, :, None, :], jnp.zeros((), jnp.bfloat16))
    masked = masked.reshape(slab_axis * CAP, slab_rows)
    partial_rent = jnp.dot(masked, slab_prices, preferred_element_type=jnp.float32)
    returned = lax.all_to_all(partial_rent.reshape(slab_axis, CAP, scenarios), "br", 0, 0, tiled=True)
    lookup = own_slab * CAP + own_slot
    fetched = jnp.take(returned.reshape(slab_axis * CAP, scenarios), lookup, axis=0)
    group_rent = jnp.sum(fetched.reshape(GDEV, list_len, scenarios), axis=1)
    return (new_injections, new_prices, group_rent)


def solution(mesh):
    placed = (
        P("br", "bus"),
        P("bus", None),
        P(("br", "bus"), None),
        P(("br", "bus")),
        P("bus"),
        P("bus"),
        P("bus"),
        P(),
        P("bus"),
        P(),
        P(),
        P(),
        P(("br", "bus"), None),
    )
    return jax.shard_map(
        per_device,
        mesh=mesh,
        in_specs=placed,
        out_specs=(P("bus", None), P(("br", "bus"), None), P(("br", "bus"), None)),
        check_vma=False,
    )
```

```python
import jax
import jax.numpy as jnp
from jax import lax
from jax.sharding import PartitionSpec as P

BLOCK = 512
CAP = 6
GDEV = 8


step_dual = 0.5
step_primal = 0.25


YHI, XR, CORES = 2, 4, 2


def bus_place():
    b = lax.axis_index("bus")
    return b // (XR * CORES), (b // CORES) % XR, b % CORES


def bus_perm(move):
    pairs = []
    for b in range(YHI * XR * CORES):
        yh, xi, c = b // (XR * CORES), (b // CORES) % XR, b % CORES
        ty, tx, tc = move(yh, xi, c)
        pairs.append((b, (ty * XR + tx) * CORES + tc))
    return pairs


CORE_SWAP = bus_perm(lambda y, x, c: (y, x, 1 - c))
X_UP = bus_perm(lambda y, x, c: (y, (x + 1) % XR, c))
X_DOWN = bus_perm(lambda y, x, c: (y, (x - 1) % XR, c))
Y_SWAP = bus_perm(lambda y, x, c: (1 - y, x, c))


def pick(a, i, axis):
    return lax.dynamic_index_in_dim(a, i, axis, keepdims=False)


def ring_scatter(parts, xi, up):
    step = 1 if up else -1
    perm = X_UP if up else X_DOWN
    acc = pick(parts, (xi - step) % XR, 0)
    for k in range(XR - 1):
        acc = lax.ppermute(acc, "bus", perm) + pick(parts, (xi - step * (k + 2)) % XR, 0)
    return acc


def ring_gather(own, xi, up):
    step = 1 if up else -1
    perm = X_UP if up else X_DOWN
    got = [own]
    for _ in range(XR - 1):
        got.append(lax.ppermute(got[-1], "bus", perm))
    stacked = jnp.stack(got)
    order = (step * (xi - jnp.arange(XR, dtype=jnp.int32))) % XR
    return jnp.take(stacked, order, axis=0)


def bus_reduce_scatter(send, keep):
    yh, xi, c = bus_place()
    y = keep + lax.ppermute(send, "bus", CORE_SWAP)
    half = y.shape[2] // 2
    cw = ring_scatter(jnp.moveaxis(y[:, :, :half], 1, 0), xi, True)
    ccw = ring_scatter(jnp.moveaxis(y[:, :, half:], 1, 0), xi, False)
    z = jnp.concatenate([cw, ccw], axis=1)
    return pick(z, yh, 0) + lax.ppermute(pick(z, 1 - yh, 0), "bus", Y_SWAP)


def bus_all_gather(p):
    yh, xi, c = bus_place()
    other = lax.ppermute(p, "bus", Y_SWAP)
    pair = jnp.where(yh == 0, jnp.stack([p, other]), jnp.stack([other, p]))
    half = p.shape[0] // 2
    cw = ring_gather(pair[:, :half], xi, True)
    ccw = ring_gather(pair[:, half:], xi, False)
    quad = jnp.moveaxis(jnp.concatenate([cw, ccw], axis=2), 0, 1)
    return quad, lax.ppermute(quad, "bus", CORE_SWAP)


def slots_of(slabs):
    positions = jnp.arange(slabs.shape[-1], dtype=jnp.int32)
    earlier = positions[None, :] < positions[:, None]
    same = slabs[..., :, None] == slabs[..., None, :]
    return jnp.sum((same & earlier).astype(jnp.int32), axis=-1)


def per_device(
    shift_factors,
    injections,
    prices,
    limits,
    unit_cost,
    bus_load,
    bus_capacity,
    irradiance_profile,
    plant_group,
    scenario_profile,
    listed_slab,
    listed_block,
    rent_weight,
):
    scenarios = injections.shape[1]
    bus_axis = lax.axis_size("bus")
    slab_axis = lax.axis_size("br")
    slab_index = lax.axis_index("br")
    column_index = lax.axis_index("bus")
    list_len = listed_slab.shape[1]
    entries = GDEV * list_len
    slab_rows = shift_factors.shape[0]
    blocks_per_slab = slab_rows // BLOCK

    slab_by_device = listed_slab.reshape(-1, entries)
    block_by_device = listed_block.reshape(-1, entries)
    self_device = slab_index * bus_axis + column_index
    own_slab = lax.dynamic_index_in_dim(slab_by_device, self_device, 0, keepdims=False)
    own_slot = slots_of(own_slab)
    slab_range = jnp.arange(slab_axis, dtype=jnp.int32)
    slot_range = jnp.arange(CAP, dtype=jnp.int32)
    pick_out = (own_slab[None, None, :] == slab_range[:, None, None]) & (
        own_slot[None, None, :] == slot_range[None, :, None]
    )
    weight_rows = rent_weight.reshape(entries, BLOCK)
    outgoing_w = jnp.einsum(
        "sce,er->scr", pick_out.astype(jnp.bfloat16), weight_rows, preferred_element_type=jnp.float32
    ).astype(jnp.bfloat16)
    arrived_w = lax.all_to_all(outgoing_w, "br", 0, 0, tiled=True)

    sources = slab_range * bus_axis + column_index
    src_slab = jnp.take(slab_by_device, sources, axis=0)
    src_block = jnp.take(block_by_device, sources, axis=0)
    src_slot = slots_of(src_slab)
    pick_in = (src_slab[:, None, :] == slab_index) & (src_slot[:, None, :] == slot_range[None, :, None])
    block_choice = jnp.sum(jnp.where(pick_in, src_block[:, None, :], 0), axis=2)
    block_hot = block_choice[:, :, None] == jnp.arange(blocks_per_slab, dtype=jnp.int32)[None, None, :]
    masked = jnp.where(block_hot[:, :, :, None], arrived_w[:, :, None, :], jnp.zeros((), jnp.bfloat16))
    yh, xi, core = bus_place()
    masked = masked.reshape(slab_axis * CAP, YHI, XR, CORES, -1)
    masked_keep = pick(masked, core, 3)
    masked_send = pick(masked, 1 - core, 3)

    bus_rows = injections.shape[0]
    share_rows = bus_rows // slab_axis
    start = slab_index * share_rows
    my_inj = lax.dynamic_slice_in_dim(injections, start, share_rows, 0)
    my_cost = lax.dynamic_slice_in_dim(unit_cost, start, share_rows, 0)
    my_load = lax.dynamic_slice_in_dim(bus_load, start, share_rows, 0)
    my_cap = lax.dynamic_slice_in_dim(bus_capacity, start, share_rows, 0)
    my_group = lax.dynamic_slice_in_dim(plant_group, start, share_rows, 0)
    by_group = jnp.take(irradiance_profile, my_group, axis=1)
    share = jnp.take(by_group, scenario_profile, axis=0).T
    upper = my_cap[:, None] * share
    lower = -my_load[:, None]
    base = my_inj - step_primal * my_cost[:, None]

    inject_half = injections.astype(jnp.bfloat16)
    by_place = shift_factors.reshape(YHI, XR, CORES, -1, shift_factors.shape[1])
    sf_keep = pick(by_place, core, 2)
    sf_send = pick(by_place, 1 - core, 2)
    flow_send = jnp.dot(sf_send, inject_half, preferred_element_type=jnp.float32)
    flow_keep = jnp.dot(sf_keep, inject_half, preferred_element_type=jnp.float32)
    flow_keep, masked_keep, masked_send, upper, lower, base = lax.optimization_barrier(
        (flow_keep, masked_keep, masked_send, upper, lower, base)
    )
    flow = bus_reduce_scatter(flow_send, flow_keep)
    moved = prices + step_dual * flow
    bound = step_dual * limits[:, None]
    new_prices = moved - jnp.clip(moved, -bound, bound)
    price_half = new_prices.astype(jnp.bfloat16)
    prices_keep, prices_send = bus_all_gather(price_half)
    contract = (((0, 1, 2), (0, 1, 2)), ((), ()))
    partial_grad = lax.dot_general(sf_keep, prices_keep, contract, preferred_element_type=jnp.float32)
    partial_grad = partial_grad + lax.dot_general(sf_send, prices_send, contract, preferred_element_type=jnp.float32)
    contract_w = (((1, 2, 3), (0, 1, 2)), ((), ()))
    partial_rent = lax.dot_general(masked_keep, prices_keep, contract_w, preferred_element_type=jnp.float32)
    partial_rent = partial_rent + lax.dot_general(masked_send, prices_send, contract_w, preferred_element_type=jnp.float32)

    outgoing = jnp.concatenate(
        [partial_grad.reshape(slab_axis, share_rows, scenarios), partial_rent.reshape(slab_axis, CAP, scenarios)], axis=1
    )
    gathered = lax.all_to_all(outgoing, "br", 0, 0, tiled=True)
    gradient = jnp.sum(gathered[:, :share_rows], axis=0)
    returned = gathered[:, share_rows:]
    trial = base - step_primal * gradient
    my_new = jnp.minimum(jnp.maximum(trial, lower), upper)
    new_injections = lax.all_to_all(
        jnp.broadcast_to(my_new[None], (slab_axis, share_rows, scenarios)), "br", 0, 0, tiled=True
    ).reshape(bus_rows, scenarios)

    lookup = own_slab * CAP + own_slot
    fetched = jnp.take(returned.reshape(slab_axis * CAP, scenarios), lookup, axis=0)
    group_rent = jnp.sum(fetched.reshape(GDEV, list_len, scenarios), axis=1)
    return (new_injections, new_prices, group_rent)


def solution(mesh):
    placed = (
        P("br", "bus"),
        P("bus", None),
        P(("br", "bus"), None),
        P(("br", "bus")),
        P("bus"),
        P("bus"),
        P("bus"),
        P(),
        P("bus"),
        P(),
        P(),
        P(),
        P(("br", "bus"), None),
    )
    return jax.shard_map(
        per_device,
        mesh=mesh,
        in_specs=placed,
        out_specs=(P("bus", None), P(("br", "bus"), None), P(("br", "bus"), None)),
        check_vma=False,
    )
```

```python
import jax
import jax.numpy as jnp
from jax import lax
from jax.sharding import PartitionSpec as P

BLOCK = 512
CAP = 6
GDEV = 8


step_dual = 0.5
step_primal = 0.25


YHI, XR, CORES = 2, 4, 2


def bus_place():
    b = lax.axis_index("bus")
    return b // (XR * CORES), (b // CORES) % XR, b % CORES


def bus_perm(move):
    pairs = []
    for b in range(YHI * XR * CORES):
        yh, xi, c = b // (XR * CORES), (b // CORES) % XR, b % CORES
        ty, tx, tc = move(yh, xi, c)
        pairs.append((b, (ty * XR + tx) * CORES + tc))
    return pairs


CORE_SWAP = bus_perm(lambda y, x, c: (y, x, 1 - c))
X_UP = bus_perm(lambda y, x, c: (y, (x + 1) % XR, c))
X_DOWN = bus_perm(lambda y, x, c: (y, (x - 1) % XR, c))
Y_SWAP = bus_perm(lambda y, x, c: (1 - y, x, c))


def pick(a, i, axis):
    return lax.dynamic_index_in_dim(a, i, axis, keepdims=False)


def ring_scatter(contribs, up):
    perm = X_UP if up else X_DOWN
    acc = contribs[0]
    for more in contribs[1:]:
        acc = lax.ppermute(acc, "bus", perm) + more
    return acc


def ring_gather(own, xi, up):
    step = 1 if up else -1
    perm = X_UP if up else X_DOWN
    got = [own]
    for _ in range(XR - 1):
        got.append(lax.ppermute(got[-1], "bus", perm))
    stacked = jnp.stack(got)
    order = (step * (xi - jnp.arange(XR, dtype=jnp.int32))) % XR
    return jnp.take(stacked, order, axis=0)


def bus_reduce_scatter(flow_part):
    yh, xi, c = bus_place()
    first = [(xi - 1) % XR, (xi + 1) % XR]
    second = [(xi + 2) % XR, xi]
    summed = []
    for group in (first, second):
        send = jnp.stack([flow_part(x, False) for x in group])
        keep = jnp.stack([flow_part(x, True) for x in group])
        summed.append(keep + lax.ppermute(send, "bus", CORE_SWAP))
    a, b = summed
    half = a.shape[2] // 2
    cw = ring_scatter([a[0, :, :half], b[0, :, :half], a[1, :, :half], b[1, :, :half]], True)
    ccw = ring_scatter([a[1, :, half:], b[0, :, half:], a[0, :, half:], b[1, :, half:]], False)
    z = jnp.concatenate([cw, ccw], axis=1)
    return z


def bus_pair_sum(z):
    yh, xi, c = bus_place()
    return pick(z, yh, 0) + lax.ppermute(pick(z, 1 - yh, 0), "bus", Y_SWAP)


def bus_all_gather(p):
    yh, xi, c = bus_place()
    other = lax.ppermute(p, "bus", Y_SWAP)
    pair = jnp.where(yh == 0, jnp.stack([p, other]), jnp.stack([other, p]))
    half = p.shape[0] // 2
    cw = ring_gather(pair[:, :half], xi, True)
    ccw = ring_gather(pair[:, half:], xi, False)
    quad = jnp.moveaxis(jnp.concatenate([cw, ccw], axis=2), 0, 1)
    return quad, lax.ppermute(quad, "bus", CORE_SWAP)


def slots_of(slabs):
    positions = jnp.arange(slabs.shape[-1], dtype=jnp.int32)
    earlier = positions[None, :] < positions[:, None]
    same = slabs[..., :, None] == slabs[..., None, :]
    return jnp.sum((same & earlier).astype(jnp.int32), axis=-1)


def per_device(
    shift_factors,
    injections,
    prices,
    limits,
    unit_cost,
    bus_load,
    bus_capacity,
    irradiance_profile,
    plant_group,
    scenario_profile,
    listed_slab,
    listed_block,
    rent_weight,
):
    scenarios = injections.shape[1]
    bus_axis = lax.axis_size("bus")
    slab_axis = lax.axis_size("br")
    slab_index = lax.axis_index("br")
    column_index = lax.axis_index("bus")
    list_len = listed_slab.shape[1]
    entries = GDEV * list_len
    slab_rows = shift_factors.shape[0]
    blocks_per_slab = slab_rows // BLOCK

    slab_by_device = listed_slab.reshape(-1, entries)
    block_by_device = listed_block.reshape(-1, entries)
    self_device = slab_index * bus_axis + column_index
    own_slab = lax.dynamic_index_in_dim(slab_by_device, self_device, 0, keepdims=False)
    own_slot = slots_of(own_slab)
    slab_range = jnp.arange(slab_axis, dtype=jnp.int32)
    slot_range = jnp.arange(CAP, dtype=jnp.int32)
    column_weights = lax.all_gather(rent_weight.reshape(entries, BLOCK), "br", axis=0, tiled=False)
    sources = slab_range * bus_axis + column_index
    src_slab = jnp.take(slab_by_device, sources, axis=0)
    src_block = jnp.take(block_by_device, sources, axis=0)
    src_slot = slots_of(src_slab)
    pick_in = (src_slab[:, None, :] == slab_index) & (src_slot[:, None, :] == slot_range[None, :, None])
    arrived_w = jnp.einsum(
        "ice,ier->icr", pick_in.astype(jnp.bfloat16), column_weights, preferred_element_type=jnp.float32
    ).astype(jnp.bfloat16)
    block_choice = jnp.sum(jnp.where(pick_in, src_block[:, None, :], 0), axis=2)
    block_hot = block_choice[:, :, None] == jnp.arange(blocks_per_slab, dtype=jnp.int32)[None, None, :]
    masked = jnp.where(block_hot[:, :, :, None], arrived_w[:, :, None, :], jnp.zeros((), jnp.bfloat16))
    yh, xi, core = bus_place()
    masked = masked.reshape(slab_axis * CAP, YHI, XR, CORES, -1)
    masked_keep = pick(masked, core, 3)
    masked_send = pick(masked, 1 - core, 3)

    bus_rows = injections.shape[0]
    share_rows = bus_rows // slab_axis
    start = slab_index * share_rows
    my_inj = lax.dynamic_slice_in_dim(injections, start, share_rows, 0)
    my_cost = lax.dynamic_slice_in_dim(unit_cost, start, share_rows, 0)
    my_load = lax.dynamic_slice_in_dim(bus_load, start, share_rows, 0)
    my_cap = lax.dynamic_slice_in_dim(bus_capacity, start, share_rows, 0)
    my_group = lax.dynamic_slice_in_dim(plant_group, start, share_rows, 0)
    by_group = jnp.take(irradiance_profile, my_group, axis=1)
    share = jnp.take(by_group, scenario_profile, axis=0).T
    upper = my_cap[:, None] * share
    lower = -my_load[:, None]
    base = my_inj - step_primal * my_cost[:, None]

    inject_half = injections.astype(jnp.bfloat16)
    by_place = shift_factors.reshape(YHI, XR, CORES, -1, shift_factors.shape[1])
    sf_keep = pick(by_place, core, 2)
    sf_send = pick(by_place, 1 - core, 2)

    def flow_part(x, mine):
        rows = pick(sf_keep if mine else sf_send, x, 1)
        return jnp.dot(rows, inject_half, preferred_element_type=jnp.float32)

    ring_out = bus_reduce_scatter(flow_part)
    ring_out, masked_keep, masked_send, upper, lower, base = lax.optimization_barrier(
        (ring_out, masked_keep, masked_send, upper, lower, base)
    )
    flow = bus_pair_sum(ring_out)
    moved = prices + step_dual * flow
    bound = step_dual * limits[:, None]
    new_prices = moved - jnp.clip(moved, -bound, bound)
    price_half = new_prices.astype(jnp.bfloat16)
    prices_keep, prices_send = bus_all_gather(price_half)
    contract = (((0, 1, 2), (0, 1, 2)), ((), ()))
    partial_grad = lax.dot_general(sf_keep, prices_keep, contract, preferred_element_type=jnp.float32)
    partial_grad = partial_grad + lax.dot_general(sf_send, prices_send, contract, preferred_element_type=jnp.float32)
    contract_w = (((1, 2, 3), (0, 1, 2)), ((), ()))
    partial_rent = lax.dot_general(masked_keep, prices_keep, contract_w, preferred_element_type=jnp.float32)
    partial_rent = partial_rent + lax.dot_general(masked_send, prices_send, contract_w, preferred_element_type=jnp.float32)

    outgoing = jnp.concatenate(
        [partial_grad.reshape(slab_axis, share_rows, scenarios), partial_rent.reshape(slab_axis, CAP, scenarios)], axis=1
    )
    gathered = lax.all_to_all(outgoing, "br", 0, 0, tiled=True)
    gradient = jnp.sum(gathered[:, :share_rows], axis=0)
    returned = gathered[:, share_rows:]
    trial = base - step_primal * gradient
    my_new = jnp.minimum(jnp.maximum(trial, lower), upper)
    new_injections = lax.all_to_all(
        jnp.broadcast_to(my_new[None], (slab_axis, share_rows, scenarios)), "br", 0, 0, tiled=True
    ).reshape(bus_rows, scenarios)

    lookup = own_slab * CAP + own_slot
    fetched = jnp.take(returned.reshape(slab_axis * CAP, scenarios), lookup, axis=0)
    group_rent = jnp.sum(fetched.reshape(GDEV, list_len, scenarios), axis=1)
    return (new_injections, new_prices, group_rent)


def solution(mesh):
    placed = (
        P("br", "bus"),
        P("bus", None),
        P(("br", "bus"), None),
        P(("br", "bus")),
        P("bus"),
        P("bus"),
        P("bus"),
        P(),
        P("bus"),
        P(),
        P(),
        P(),
        P(("br", "bus"), None),
    )
    return jax.shard_map(
        per_device,
        mesh=mesh,
        in_specs=placed,
        out_specs=(P("bus", None), P(("br", "bus"), None), P(("br", "bus"), None)),
        check_vma=False,
    )
```

```python
import jax
import jax.numpy as jnp
from jax import lax
from jax.sharding import PartitionSpec as P

BLOCK = 512
CAP = 6
GDEV = 8


step_dual = 0.5
step_primal = 0.25


YHI, XR, CORES = 2, 4, 2


def bus_place():
    b = lax.axis_index("bus")
    return b // (XR * CORES), (b // CORES) % XR, b % CORES


def bus_perm(move):
    pairs = []
    for b in range(YHI * XR * CORES):
        yh, xi, c = b // (XR * CORES), (b // CORES) % XR, b % CORES
        ty, tx, tc = move(yh, xi, c)
        pairs.append((b, (ty * XR + tx) * CORES + tc))
    return pairs


CORE_SWAP = bus_perm(lambda y, x, c: (y, x, 1 - c))
X_UP = bus_perm(lambda y, x, c: (y, (x + 1) % XR, c))
X_DOWN = bus_perm(lambda y, x, c: (y, (x - 1) % XR, c))
Y_SWAP = bus_perm(lambda y, x, c: (1 - y, x, c))


def pick(a, i, axis):
    return lax.dynamic_index_in_dim(a, i, axis, keepdims=False)


def ring_scatter(contribs, up):
    perm = X_UP if up else X_DOWN
    acc = contribs[0]
    for more in contribs[1:]:
        acc = lax.ppermute(acc, "bus", perm) + more
    return acc


def ring_gather(own, xi, up):
    step = 1 if up else -1
    perm = X_UP if up else X_DOWN
    out = jnp.zeros((XR,) + own.shape, own.dtype)
    cur = own
    for m in range(XR):
        if m:
            cur = lax.ppermute(cur, "bus", perm)
        out = lax.dynamic_update_index_in_dim(out, cur, (xi - step * m) % XR, 0)
    return out


def bus_reduce_scatter(flow_part):
    yh, xi, c = bus_place()
    first = [(xi - 1) % XR, (xi + 1) % XR]
    second = [(xi + 2) % XR, xi]
    summed = []
    for group in (first, second):
        send = tuple(flow_part(x, False) for x in group)
        keep = tuple(flow_part(x, True) for x in group)
        came = lax.ppermute(send, "bus", CORE_SWAP)
        summed.append([k + r for k, r in zip(keep, came)])
    (a0, a1), (b0, b1) = summed
    half = a0.shape[1] // 2
    cw = ring_scatter([a0[:, :half], b0[:, :half], a1[:, :half], b1[:, :half]], True)
    ccw = ring_scatter([a1[:, half:], b0[:, half:], a0[:, half:], b1[:, half:]], False)
    z = jnp.concatenate([cw, ccw], axis=1)
    return z


def bus_pair_sum(z):
    yh, xi, c = bus_place()
    return pick(z, yh, 0) + lax.ppermute(pick(z, 1 - yh, 0), "bus", Y_SWAP)


def bus_all_gather(p):
    yh, xi, c = bus_place()
    other = lax.ppermute(p, "bus", Y_SWAP)
    pair = jnp.where(yh == 0, jnp.stack([p, other]), jnp.stack([other, p]))
    half = p.shape[0] // 2
    cw = ring_gather(pair[:, :half], xi, True)
    ccw = ring_gather(pair[:, half:], xi, False)
    quad = jnp.moveaxis(jnp.concatenate([cw, ccw], axis=2), 0, 1)
    return quad, lax.ppermute(quad, "bus", CORE_SWAP)


def slots_of(slabs):
    positions = jnp.arange(slabs.shape[-1], dtype=jnp.int32)
    earlier = positions[None, :] < positions[:, None]
    same = slabs[..., :, None] == slabs[..., None, :]
    return jnp.sum((same & earlier).astype(jnp.int32), axis=-1)


def per_device(
    shift_factors,
    injections,
    prices,
    limits,
    unit_cost,
    bus_load,
    bus_capacity,
    irradiance_profile,
    plant_group,
    scenario_profile,
    listed_slab,
    listed_block,
    rent_weight,
):
    scenarios = injections.shape[1]
    bus_axis = lax.axis_size("bus")
    slab_axis = lax.axis_size("br")
    slab_index = lax.axis_index("br")
    column_index = lax.axis_index("bus")
    list_len = listed_slab.shape[1]
    entries = GDEV * list_len
    slab_rows = shift_factors.shape[0]
    blocks_per_slab = slab_rows // BLOCK

    yh, xi, core = bus_place()
    inject_half = injections.astype(jnp.bfloat16)
    by_place = shift_factors.reshape(YHI, XR, CORES, -1, shift_factors.shape[1])
    sf_keep = pick(by_place, core, 2)
    sf_send = pick(by_place, 1 - core, 2)

    def flow_part(x, mine):
        rows = pick(sf_keep if mine else sf_send, x, 1)
        return jnp.dot(rows, inject_half, preferred_element_type=jnp.float32)

    ring_out = bus_reduce_scatter(flow_part)
    inputs_after = (listed_slab, listed_block, rent_weight, irradiance_profile, plant_group, scenario_profile)
    ring_out, inputs_after = lax.optimization_barrier((ring_out, inputs_after))
    listed_slab, listed_block, rent_weight, irradiance_profile, plant_group, scenario_profile = inputs_after

    slab_by_device = listed_slab.reshape(-1, entries)
    block_by_device = listed_block.reshape(-1, entries)
    self_device = slab_index * bus_axis + column_index
    own_slab = lax.dynamic_index_in_dim(slab_by_device, self_device, 0, keepdims=False)
    own_slot = slots_of(own_slab)
    slab_range = jnp.arange(slab_axis, dtype=jnp.int32)
    slot_range = jnp.arange(CAP, dtype=jnp.int32)
    pick_out = (own_slab[None, None, :] == slab_range[:, None, None]) & (
        own_slot[None, None, :] == slot_range[None, :, None]
    )
    weight_rows = rent_weight.reshape(entries, BLOCK)
    outgoing_w = jnp.einsum(
        "sce,er->scr", pick_out.astype(jnp.bfloat16), weight_rows, preferred_element_type=jnp.float32
    ).astype(jnp.bfloat16)
    arrived_w = lax.all_to_all(outgoing_w, "br", 0, 0, tiled=True)

    sources = slab_range * bus_axis + column_index
    src_slab = jnp.take(slab_by_device, sources, axis=0)
    src_block = jnp.take(block_by_device, sources, axis=0)
    src_slot = slots_of(src_slab)
    pick_in = (src_slab[:, None, :] == slab_index) & (src_slot[:, None, :] == slot_range[None, :, None])
    block_choice = jnp.sum(jnp.where(pick_in, src_block[:, None, :], 0), axis=2)
    block_hot = block_choice[:, :, None] == jnp.arange(blocks_per_slab, dtype=jnp.int32)[None, None, :]
    masked = jnp.where(block_hot[:, :, :, None], arrived_w[:, :, None, :], jnp.zeros((), jnp.bfloat16))
    masked = masked.reshape(slab_axis * CAP, YHI, XR, CORES, -1)
    masked_keep = pick(masked, core, 3)
    masked_send = pick(masked, 1 - core, 3)

    bus_rows = injections.shape[0]
    share_rows = bus_rows // slab_axis
    start = slab_index * share_rows
    my_inj = lax.dynamic_slice_in_dim(injections, start, share_rows, 0)
    my_cost = lax.dynamic_slice_in_dim(unit_cost, start, share_rows, 0)
    my_load = lax.dynamic_slice_in_dim(bus_load, start, share_rows, 0)
    my_cap = lax.dynamic_slice_in_dim(bus_capacity, start, share_rows, 0)
    my_group = lax.dynamic_slice_in_dim(plant_group, start, share_rows, 0)
    by_group = jnp.take(irradiance_profile, my_group, axis=1)
    share = jnp.take(by_group, scenario_profile, axis=0).T
    upper = my_cap[:, None] * share
    lower = -my_load[:, None]
    base = my_inj - step_primal * my_cost[:, None]

    flow = bus_pair_sum(ring_out)
    moved = prices + step_dual * flow
    bound = step_dual * limits[:, None]
    new_prices = moved - jnp.clip(moved, -bound, bound)
    price_half = new_prices.astype(jnp.bfloat16)
    prices_keep, prices_send = bus_all_gather(price_half)
    contract = (((0, 1, 2), (0, 1, 2)), ((), ()))
    partial_grad = lax.dot_general(sf_keep, prices_keep, contract, preferred_element_type=jnp.float32)
    partial_grad = partial_grad + lax.dot_general(sf_send, prices_send, contract, preferred_element_type=jnp.float32)
    contract_w = (((1, 2, 3), (0, 1, 2)), ((), ()))
    partial_rent = lax.dot_general(masked_keep, prices_keep, contract_w, preferred_element_type=jnp.float32)
    partial_rent = partial_rent + lax.dot_general(masked_send, prices_send, contract_w, preferred_element_type=jnp.float32)

    outgoing = jnp.concatenate(
        [partial_grad.reshape(slab_axis, share_rows, scenarios), partial_rent.reshape(slab_axis, CAP, scenarios)], axis=1
    )
    gathered = lax.all_to_all(outgoing, "br", 0, 0, tiled=True)
    gradient = jnp.sum(gathered[:, :share_rows], axis=0)
    returned = gathered[:, share_rows:]
    trial = base - step_primal * gradient
    my_new = jnp.minimum(jnp.maximum(trial, lower), upper)
    new_injections = lax.all_to_all(
        jnp.broadcast_to(my_new[None], (slab_axis, share_rows, scenarios)), "br", 0, 0, tiled=True
    ).reshape(bus_rows, scenarios)

    lookup = own_slab * CAP + own_slot
    fetched = jnp.take(returned.reshape(slab_axis * CAP, scenarios), lookup, axis=0)
    group_rent = jnp.sum(fetched.reshape(GDEV, list_len, scenarios), axis=1)
    return (new_injections, new_prices, group_rent)


def solution(mesh):
    placed = (
        P("br", "bus"),
        P("bus", None),
        P(("br", "bus"), None),
        P(("br", "bus")),
        P("bus"),
        P("bus"),
        P("bus"),
        P(),
        P("bus"),
        P(),
        P(),
        P(),
        P(("br", "bus"), None),
    )
    return jax.shard_map(
        per_device,
        mesh=mesh,
        in_specs=placed,
        out_specs=(P("bus", None), P(("br", "bus"), None), P(("br", "bus"), None)),
        check_vma=False,
    )
```

```python
import jax
import jax.numpy as jnp
from jax import lax
from jax.sharding import PartitionSpec as P

BLOCK = 512
CAP = 6
GDEV = 8


step_dual = 0.5
step_primal = 0.25


YHI, XR, CORES = 2, 4, 2


def bus_place():
    b = lax.axis_index("bus")
    return b // (XR * CORES), (b // CORES) % XR, b % CORES


def bus_perm(move):
    pairs = []
    for b in range(YHI * XR * CORES):
        yh, xi, c = b // (XR * CORES), (b // CORES) % XR, b % CORES
        ty, tx, tc = move(yh, xi, c)
        pairs.append((b, (ty * XR + tx) * CORES + tc))
    return pairs


CORE_SWAP = bus_perm(lambda y, x, c: (y, x, 1 - c))
X_UP = bus_perm(lambda y, x, c: (y, (x + 1) % XR, c))
X_DOWN = bus_perm(lambda y, x, c: (y, (x - 1) % XR, c))
Y_SWAP = bus_perm(lambda y, x, c: (1 - y, x, c))


def pick(a, i, axis):
    return lax.dynamic_index_in_dim(a, i, axis, keepdims=False)


def ring_scatter(contribs, up):
    perm = X_UP if up else X_DOWN
    acc = contribs[0]
    for more in contribs[1:]:
        acc = lax.ppermute(acc, "bus", perm) + more
    return acc


def ring_gather(own, xi, up):
    step = 1 if up else -1
    perm = X_UP if up else X_DOWN
    out = jnp.zeros((XR,) + own.shape, own.dtype)
    cur = own
    for m in range(XR):
        if m:
            cur = lax.ppermute(cur, "bus", perm)
        out = lax.dynamic_update_index_in_dim(out, cur, (xi - step * m) % XR, 0)
    return out


def bus_reduce_scatter(flow_part):
    yh, xi, c = bus_place()
    first = [(xi - 1) % XR, (xi + 1) % XR]
    second = [(xi + 2) % XR, xi]
    summed = []
    for group in (first, second):
        send = jnp.stack([flow_part(x, False) for x in group])
        keep = jnp.stack([flow_part(x, True) for x in group])
        summed.append(keep + lax.ppermute(send, "bus", CORE_SWAP))
    a, b = summed
    half = a.shape[2] // 2
    cw = ring_scatter([a[0, :, :half], b[0, :, :half], a[1, :, :half], b[1, :, :half]], True)
    ccw = ring_scatter([a[1, :, half:], b[0, :, half:], a[0, :, half:], b[1, :, half:]], False)
    z = jnp.concatenate([cw, ccw], axis=1)
    return z


def bus_pair_sum(z):
    yh, xi, c = bus_place()
    return pick(z, yh, 0) + lax.ppermute(pick(z, 1 - yh, 0), "bus", Y_SWAP)


def bus_all_gather(p):
    yh, xi, c = bus_place()
    other = lax.ppermute(p, "bus", Y_SWAP)
    pair = jnp.where(yh == 0, jnp.stack([p, other]), jnp.stack([other, p]))
    half = p.shape[0] // 2
    cw = ring_gather(pair[:, :half], xi, True)
    ccw = ring_gather(pair[:, half:], xi, False)
    quad = jnp.moveaxis(jnp.concatenate([cw, ccw], axis=2), 0, 1)
    return quad, lax.ppermute(quad, "bus", CORE_SWAP)


def slots_of(slabs):
    positions = jnp.arange(slabs.shape[-1], dtype=jnp.int32)
    earlier = positions[None, :] < positions[:, None]
    same = slabs[..., :, None] == slabs[..., None, :]
    return jnp.sum((same & earlier).astype(jnp.int32), axis=-1)


def per_device(
    shift_factors,
    injections,
    prices,
    limits,
    unit_cost,
    bus_load,
    bus_capacity,
    irradiance_profile,
    plant_group,
    scenario_profile,
    listed_slab,
    listed_block,
    rent_weight,
):
    scenarios = injections.shape[1]
    bus_axis = lax.axis_size("bus")
    slab_axis = lax.axis_size("br")
    slab_index = lax.axis_index("br")
    column_index = lax.axis_index("bus")
    list_len = listed_slab.shape[1]
    entries = GDEV * list_len
    slab_rows = shift_factors.shape[0]
    blocks_per_slab = slab_rows // BLOCK

    slab_by_device = listed_slab.reshape(-1, entries)
    block_by_device = listed_block.reshape(-1, entries)
    self_device = slab_index * bus_axis + column_index
    own_slab = lax.dynamic_index_in_dim(slab_by_device, self_device, 0, keepdims=False)
    own_slot = slots_of(own_slab)
    slab_range = jnp.arange(slab_axis, dtype=jnp.int32)
    slot_range = jnp.arange(CAP, dtype=jnp.int32)
    pick_out = (own_slab[None, None, :] == slab_range[:, None, None]) & (
        own_slot[None, None, :] == slot_range[None, :, None]
    )
    weight_rows = rent_weight.reshape(entries, BLOCK)
    outgoing_w = jnp.einsum(
        "sce,er->scr", pick_out.astype(jnp.bfloat16), weight_rows, preferred_element_type=jnp.float32
    ).astype(jnp.bfloat16)
    arrived_w = lax.all_to_all(outgoing_w, "br", 0, 0, tiled=True)
    sources = slab_range * bus_axis + column_index
    src_slab = jnp.take(slab_by_device, sources, axis=0)
    src_block = jnp.take(block_by_device, sources, axis=0)
    src_slot = slots_of(src_slab)
    pick_in = (src_slab[:, None, :] == slab_index) & (src_slot[:, None, :] == slot_range[None, :, None])
    block_choice = jnp.sum(jnp.where(pick_in, src_block[:, None, :], 0), axis=2)
    block_hot = block_choice[:, :, None] == jnp.arange(blocks_per_slab, dtype=jnp.int32)[None, None, :]
    masked = jnp.where(block_hot[:, :, :, None], arrived_w[:, :, None, :], jnp.zeros((), jnp.bfloat16))
    yh, xi, core = bus_place()
    masked = masked.reshape(slab_axis * CAP, YHI, XR, CORES, -1)
    masked_keep = pick(masked, core, 3)
    masked_send = pick(masked, 1 - core, 3)

    bus_rows = injections.shape[0]
    share_rows = bus_rows // slab_axis
    start = slab_index * share_rows
    my_inj = lax.dynamic_slice_in_dim(injections, start, share_rows, 0)
    my_cost = lax.dynamic_slice_in_dim(unit_cost, start, share_rows, 0)
    my_load = lax.dynamic_slice_in_dim(bus_load, start, share_rows, 0)
    my_cap = lax.dynamic_slice_in_dim(bus_capacity, start, share_rows, 0)
    my_group = lax.dynamic_slice_in_dim(plant_group, start, share_rows, 0)
    by_group = jnp.take(irradiance_profile, my_group, axis=1)
    share = jnp.take(by_group, scenario_profile, axis=0).T
    upper = my_cap[:, None] * share
    lower = -my_load[:, None]
    base = my_inj - step_primal * my_cost[:, None]

    inject_half = injections.astype(jnp.bfloat16)
    by_place = shift_factors.reshape(YHI, XR, CORES, -1, shift_factors.shape[1])
    sf_keep = pick(by_place, core, 2)
    sf_send = pick(by_place, 1 - core, 2)

    def flow_part(x, mine):
        rows = pick(sf_keep if mine else sf_send, x, 1)
        return jnp.dot(rows, inject_half, preferred_element_type=jnp.float32)

    ring_out = bus_reduce_scatter(flow_part)
    ring_out, masked_keep, masked_send, upper, lower, base = lax.optimization_barrier(
        (ring_out, masked_keep, masked_send, upper, lower, base)
    )
    flow = bus_pair_sum(ring_out)
    moved = prices + step_dual * flow
    bound = step_dual * limits[:, None]
    new_prices = moved - jnp.clip(moved, -bound, bound)
    price_half = new_prices.astype(jnp.bfloat16)
    prices_keep, prices_send = bus_all_gather(price_half)
    contract = (((0, 1, 2), (0, 1, 2)), ((), ()))
    partial_grad = lax.dot_general(sf_keep, prices_keep, contract, preferred_element_type=jnp.float32)
    partial_grad = partial_grad + lax.dot_general(sf_send, prices_send, contract, preferred_element_type=jnp.float32)
    contract_w = (((1, 2, 3), (0, 1, 2)), ((), ()))
    partial_rent = lax.dot_general(masked_keep, prices_keep, contract_w, preferred_element_type=jnp.float32)
    partial_rent = partial_rent + lax.dot_general(masked_send, prices_send, contract_w, preferred_element_type=jnp.float32)

    outgoing = jnp.concatenate(
        [partial_grad.reshape(slab_axis, share_rows, scenarios), partial_rent.reshape(slab_axis, CAP, scenarios)], axis=1
    )
    gathered = lax.all_to_all(outgoing, "br", 0, 0, tiled=True)
    gradient = jnp.sum(gathered[:, :share_rows], axis=0)
    returned = gathered[:, share_rows:]
    trial = base - step_primal * gradient
    my_new = jnp.minimum(jnp.maximum(trial, lower), upper)
    new_injections = lax.all_to_all(
        jnp.broadcast_to(my_new[None], (slab_axis, share_rows, scenarios)), "br", 0, 0, tiled=True
    ).reshape(bus_rows, scenarios)

    lookup = own_slab * CAP + own_slot
    fetched = jnp.take(returned.reshape(slab_axis * CAP, scenarios), lookup, axis=0)
    group_rent = jnp.sum(fetched.reshape(GDEV, list_len, scenarios), axis=1)
    return (new_injections, new_prices, group_rent)


def solution(mesh):
    placed = (
        P("br", "bus"),
        P("bus", None),
        P(("br", "bus"), None),
        P(("br", "bus")),
        P("bus"),
        P("bus"),
        P("bus"),
        P(),
        P("bus"),
        P(),
        P(),
        P(),
        P(("br", "bus"), None),
    )
    return jax.shard_map(
        per_device,
        mesh=mesh,
        in_specs=placed,
        out_specs=(P("bus", None), P(("br", "bus"), None), P(("br", "bus"), None)),
        check_vma=False,
    )
```

```python
import jax
import jax.numpy as jnp
from jax import lax
from jax.sharding import PartitionSpec as P

BLOCK = 512
CAP = 6
GDEV = 8


step_dual = 0.5
step_primal = 0.25


YHI, XR, CORES = 2, 4, 2


def bus_place():
    b = lax.axis_index("bus")
    return b // (XR * CORES), (b // CORES) % XR, b % CORES


def bus_perm(move):
    pairs = []
    for b in range(YHI * XR * CORES):
        yh, xi, c = b // (XR * CORES), (b // CORES) % XR, b % CORES
        ty, tx, tc = move(yh, xi, c)
        pairs.append((b, (ty * XR + tx) * CORES + tc))
    return pairs


CORE_SWAP = bus_perm(lambda y, x, c: (y, x, 1 - c))
X_UP = bus_perm(lambda y, x, c: (y, (x + 1) % XR, c))
X_DOWN = bus_perm(lambda y, x, c: (y, (x - 1) % XR, c))
Y_SWAP = bus_perm(lambda y, x, c: (1 - y, x, c))


def pick(a, i, axis):
    return lax.dynamic_index_in_dim(a, i, axis, keepdims=False)


def ring_scatter(contribs, up, rider=None):
    perm = X_UP if up else X_DOWN
    acc = contribs[0]
    for k, more in enumerate(contribs[1:]):
        acc = lax.ppermute(acc, "bus", perm) + more
        if k == 0 and rider is not None:
            acc, rider = lax.optimization_barrier((acc, rider))
    return acc, rider


def ring_gather(own, xi, up):
    step = 1 if up else -1
    perm = X_UP if up else X_DOWN
    out = jnp.zeros((XR,) + own.shape, own.dtype)
    cur = own
    for m in range(XR):
        if m:
            cur = lax.ppermute(cur, "bus", perm)
        out = lax.dynamic_update_index_in_dim(out, cur, (xi - step * m) % XR, 0)
    return out


def bus_reduce_scatter(flow_part, rider):
    yh, xi, c = bus_place()
    first = [(xi - 1) % XR, (xi + 1) % XR]
    second = [(xi + 2) % XR, xi]
    summed = []
    for group in (first, second):
        send = jnp.stack([flow_part(x, False) for x in group])
        keep = jnp.stack([flow_part(x, True) for x in group])
        summed.append(keep + lax.ppermute(send, "bus", CORE_SWAP))
    a, b = summed
    half = a.shape[2] // 2
    cw, rider = ring_scatter([a[0, :, :half], b[0, :, :half], a[1, :, :half], b[1, :, :half]], True, rider)
    ccw, _ = ring_scatter([a[1, :, half:], b[0, :, half:], a[0, :, half:], b[1, :, half:]], False)
    z = jnp.concatenate([cw, ccw], axis=1)
    return z, rider


def bus_pair_sum(z):
    yh, xi, c = bus_place()
    return pick(z, yh, 0) + lax.ppermute(pick(z, 1 - yh, 0), "bus", Y_SWAP)


def bus_all_gather(p):
    yh, xi, c = bus_place()
    other = lax.ppermute(p, "bus", Y_SWAP)
    pair = jnp.where(yh == 0, jnp.stack([p, other]), jnp.stack([other, p]))
    half = p.shape[0] // 2
    cw = ring_gather(pair[:, :half], xi, True)
    ccw = ring_gather(pair[:, half:], xi, False)
    quad = jnp.moveaxis(jnp.concatenate([cw, ccw], axis=2), 0, 1)
    return quad, lax.ppermute(quad, "bus", CORE_SWAP)


def slots_of(slabs):
    positions = jnp.arange(slabs.shape[-1], dtype=jnp.int32)
    earlier = positions[None, :] < positions[:, None]
    same = slabs[..., :, None] == slabs[..., None, :]
    return jnp.sum((same & earlier).astype(jnp.int32), axis=-1)


def per_device(
    shift_factors,
    injections,
    prices,
    limits,
    unit_cost,
    bus_load,
    bus_capacity,
    irradiance_profile,
    plant_group,
    scenario_profile,
    listed_slab,
    listed_block,
    rent_weight,
):
    scenarios = injections.shape[1]
    bus_axis = lax.axis_size("bus")
    slab_axis = lax.axis_size("br")
    slab_index = lax.axis_index("br")
    column_index = lax.axis_index("bus")
    list_len = listed_slab.shape[1]
    entries = GDEV * list_len
    slab_rows = shift_factors.shape[0]
    blocks_per_slab = slab_rows // BLOCK

    slab_by_device = listed_slab.reshape(-1, entries)
    block_by_device = listed_block.reshape(-1, entries)
    self_device = slab_index * bus_axis + column_index
    own_slab = lax.dynamic_index_in_dim(slab_by_device, self_device, 0, keepdims=False)
    own_slot = slots_of(own_slab)
    slab_range = jnp.arange(slab_axis, dtype=jnp.int32)
    slot_range = jnp.arange(CAP, dtype=jnp.int32)
    pick_out = (own_slab[None, None, :] == slab_range[:, None, None]) & (
        own_slot[None, None, :] == slot_range[None, :, None]
    )
    weight_rows = rent_weight.reshape(entries, BLOCK)
    outgoing_w = jnp.einsum(
        "sce,er->scr", pick_out.astype(jnp.bfloat16), weight_rows, preferred_element_type=jnp.float32
    ).astype(jnp.bfloat16)
    sources = slab_range * bus_axis + column_index
    src_slab = jnp.take(slab_by_device, sources, axis=0)
    src_block = jnp.take(block_by_device, sources, axis=0)
    src_slot = slots_of(src_slab)
    pick_in = (src_slab[:, None, :] == slab_index) & (src_slot[:, None, :] == slot_range[None, :, None])
    block_choice = jnp.sum(jnp.where(pick_in, src_block[:, None, :], 0), axis=2)
    block_hot = block_choice[:, :, None] == jnp.arange(blocks_per_slab, dtype=jnp.int32)[None, None, :]
    yh, xi, core = bus_place()

    bus_rows = injections.shape[0]
    share_rows = bus_rows // slab_axis
    start = slab_index * share_rows
    my_inj = lax.dynamic_slice_in_dim(injections, start, share_rows, 0)
    my_cost = lax.dynamic_slice_in_dim(unit_cost, start, share_rows, 0)
    my_load = lax.dynamic_slice_in_dim(bus_load, start, share_rows, 0)
    my_cap = lax.dynamic_slice_in_dim(bus_capacity, start, share_rows, 0)
    my_group = lax.dynamic_slice_in_dim(plant_group, start, share_rows, 0)
    by_group = jnp.take(irradiance_profile, my_group, axis=1)
    share = jnp.take(by_group, scenario_profile, axis=0).T
    upper = my_cap[:, None] * share
    lower = -my_load[:, None]
    base = my_inj - step_primal * my_cost[:, None]

    inject_half = injections.astype(jnp.bfloat16)
    by_place = shift_factors.reshape(YHI, XR, CORES, -1, shift_factors.shape[1])
    sf_keep = pick(by_place, core, 2)
    sf_send = pick(by_place, 1 - core, 2)

    def flow_part(x, mine):
        rows = pick(sf_keep if mine else sf_send, x, 1)
        return jnp.dot(rows, inject_half, preferred_element_type=jnp.float32)

    ring_out, outgoing_w = bus_reduce_scatter(flow_part, outgoing_w)
    arrived_w = lax.all_to_all(outgoing_w, "br", 0, 0, tiled=True)
    masked = jnp.where(block_hot[:, :, :, None], arrived_w[:, :, None, :], jnp.zeros((), jnp.bfloat16))
    masked = masked.reshape(slab_axis * CAP, YHI, XR, CORES, -1)
    masked_keep = pick(masked, core, 3)
    masked_send = pick(masked, 1 - core, 3)
    ring_out, masked_keep, masked_send, upper, lower, base = lax.optimization_barrier(
        (ring_out, masked_keep, masked_send, upper, lower, base)
    )
    flow = bus_pair_sum(ring_out)
    moved = prices + step_dual * flow
    bound = step_dual * limits[:, None]
    new_prices = moved - jnp.clip(moved, -bound, bound)
    price_half = new_prices.astype(jnp.bfloat16)
    prices_keep, prices_send = bus_all_gather(price_half)
    contract = (((0, 1, 2), (0, 1, 2)), ((), ()))
    partial_grad = lax.dot_general(sf_keep, prices_keep, contract, preferred_element_type=jnp.float32)
    partial_grad = partial_grad + lax.dot_general(sf_send, prices_send, contract, preferred_element_type=jnp.float32)
    contract_w = (((1, 2, 3), (0, 1, 2)), ((), ()))
    partial_rent = lax.dot_general(masked_keep, prices_keep, contract_w, preferred_element_type=jnp.float32)
    partial_rent = partial_rent + lax.dot_general(masked_send, prices_send, contract_w, preferred_element_type=jnp.float32)

    gathered = lax.all_to_all(partial_grad.reshape(slab_axis, share_rows, scenarios), "br", 0, 0, tiled=True)
    returned = lax.all_to_all(partial_rent.reshape(slab_axis, CAP, scenarios), "br", 0, 0, tiled=True)
    gradient = jnp.sum(gathered, axis=0)
    trial = base - step_primal * gradient
    my_new = jnp.minimum(jnp.maximum(trial, lower), upper)
    new_injections = lax.all_to_all(
        jnp.broadcast_to(my_new[None], (slab_axis, share_rows, scenarios)), "br", 0, 0, tiled=True
    ).reshape(bus_rows, scenarios)

    lookup = own_slab * CAP + own_slot
    fetched = jnp.take(returned.reshape(slab_axis * CAP, scenarios), lookup, axis=0)
    group_rent = jnp.sum(fetched.reshape(GDEV, list_len, scenarios), axis=1)
    return (new_injections, new_prices, group_rent)


def solution(mesh):
    placed = (
        P("br", "bus"),
        P("bus", None),
        P(("br", "bus"), None),
        P(("br", "bus")),
        P("bus"),
        P("bus"),
        P("bus"),
        P(),
        P("bus"),
        P(),
        P(),
        P(),
        P(("br", "bus"), None),
    )
    return jax.shard_map(
        per_device,
        mesh=mesh,
        in_specs=placed,
        out_specs=(P("bus", None), P(("br", "bus"), None), P(("br", "bus"), None)),
        check_vma=False,
    )
```

```python
import jax
import jax.numpy as jnp
from jax import lax
from jax.sharding import PartitionSpec as P

BLOCK = 512
CAP = 6
GDEV = 8


step_dual = 0.5
step_primal = 0.25


YHI, XR, CORES = 2, 4, 2


def bus_place():
    b = lax.axis_index("bus")
    return b // (XR * CORES), (b // CORES) % XR, b % CORES


def bus_perm(move):
    pairs = []
    for b in range(YHI * XR * CORES):
        yh, xi, c = b // (XR * CORES), (b // CORES) % XR, b % CORES
        ty, tx, tc = move(yh, xi, c)
        pairs.append((b, (ty * XR + tx) * CORES + tc))
    return pairs


CORE_SWAP = bus_perm(lambda y, x, c: (y, x, 1 - c))
X_UP = bus_perm(lambda y, x, c: (y, (x + 1) % XR, c))
X_DOWN = bus_perm(lambda y, x, c: (y, (x - 1) % XR, c))
Y_SWAP = bus_perm(lambda y, x, c: (1 - y, x, c))


def pick(a, i, axis):
    return lax.dynamic_index_in_dim(a, i, axis, keepdims=False)


def ring_scatter(contribs, up, rider=None):
    perm = X_UP if up else X_DOWN
    acc = contribs[0]
    for k, more in enumerate(contribs[1:]):
        acc = lax.ppermute(acc, "bus", perm) + more
        if k == 0 and rider is not None:
            acc, rider = lax.optimization_barrier((acc, rider))
    return acc, rider


def ring_gather(own, xi, up):
    step = 1 if up else -1
    perm = X_UP if up else X_DOWN
    out = jnp.zeros((XR,) + own.shape, own.dtype)
    cur = own
    for m in range(XR):
        if m:
            cur = lax.ppermute(cur, "bus", perm)
        out = lax.dynamic_update_index_in_dim(out, cur, (xi - step * m) % XR, 0)
    return out


def bus_reduce_scatter(flow_part, rider):
    yh, xi, c = bus_place()
    first = [(xi - 1) % XR, (xi + 1) % XR]
    second = [(xi + 2) % XR, xi]
    summed = []
    for group in (first, second):
        send = jnp.stack([flow_part(x, False) for x in group])
        keep = jnp.stack([flow_part(x, True) for x in group])
        summed.append(keep + lax.ppermute(send, "bus", CORE_SWAP))
    a, b = summed
    half = a.shape[2] // 2
    cw, rider = ring_scatter([a[0, :, :half], b[0, :, :half], a[1, :, :half], b[1, :, :half]], True, rider)
    ccw, _ = ring_scatter([a[1, :, half:], b[0, :, half:], a[0, :, half:], b[1, :, half:]], False)
    z = jnp.concatenate([cw, ccw], axis=1)
    return z, rider


def bus_pair_sum(z):
    yh, xi, c = bus_place()
    return pick(z, yh, 0) + lax.ppermute(pick(z, 1 - yh, 0), "bus", Y_SWAP)


def bus_all_gather(p):
    yh, xi, c = bus_place()
    other = lax.ppermute(p, "bus", Y_SWAP)
    pair = jnp.where(yh == 0, jnp.stack([p, other]), jnp.stack([other, p]))
    half = p.shape[0] // 2
    cw = ring_gather(pair[:, :half], xi, True)
    ccw = ring_gather(pair[:, half:], xi, False)
    quad = jnp.moveaxis(jnp.concatenate([cw, ccw], axis=2), 0, 1)
    return quad, lax.ppermute(quad, "bus", CORE_SWAP)


def slots_of(slabs):
    positions = jnp.arange(slabs.shape[-1], dtype=jnp.int32)
    earlier = positions[None, :] < positions[:, None]
    same = slabs[..., :, None] == slabs[..., None, :]
    return jnp.sum((same & earlier).astype(jnp.int32), axis=-1)


def per_device(
    shift_factors,
    injections,
    prices,
    limits,
    unit_cost,
    bus_load,
    bus_capacity,
    irradiance_profile,
    plant_group,
    scenario_profile,
    listed_slab,
    listed_block,
    rent_weight,
):
    scenarios = injections.shape[1]
    bus_axis = lax.axis_size("bus")
    slab_axis = lax.axis_size("br")
    slab_index = lax.axis_index("br")
    column_index = lax.axis_index("bus")
    list_len = listed_slab.shape[1]
    entries = GDEV * list_len
    slab_rows = shift_factors.shape[0]
    blocks_per_slab = slab_rows // BLOCK

    slab_by_device = listed_slab.reshape(-1, entries)
    block_by_device = listed_block.reshape(-1, entries)
    self_device = slab_index * bus_axis + column_index
    own_slab = lax.dynamic_index_in_dim(slab_by_device, self_device, 0, keepdims=False)
    own_slot = slots_of(own_slab)
    slab_range = jnp.arange(slab_axis, dtype=jnp.int32)
    slot_range = jnp.arange(CAP, dtype=jnp.int32)
    pick_out = (own_slab[None, None, :] == slab_range[:, None, None]) & (
        own_slot[None, None, :] == slot_range[None, :, None]
    )
    weight_rows = rent_weight.reshape(entries, BLOCK)
    outgoing_w = jnp.einsum(
        "sce,er->scr", pick_out.astype(jnp.bfloat16), weight_rows, preferred_element_type=jnp.float32
    ).astype(jnp.bfloat16)
    sources = slab_range * bus_axis + column_index
    src_slab = jnp.take(slab_by_device, sources, axis=0)
    src_block = jnp.take(block_by_device, sources, axis=0)
    src_slot = slots_of(src_slab)
    pick_in = (src_slab[:, None, :] == slab_index) & (src_slot[:, None, :] == slot_range[None, :, None])
    block_choice = jnp.sum(jnp.where(pick_in, src_block[:, None, :], 0), axis=2)
    block_hot = block_choice[:, :, None] == jnp.arange(blocks_per_slab, dtype=jnp.int32)[None, None, :]
    yh, xi, core = bus_place()

    bus_rows = injections.shape[0]
    share_rows = bus_rows // slab_axis
    start = slab_index * share_rows
    my_inj = lax.dynamic_slice_in_dim(injections, start, share_rows, 0)
    my_cost = lax.dynamic_slice_in_dim(unit_cost, start, share_rows, 0)
    my_load = lax.dynamic_slice_in_dim(bus_load, start, share_rows, 0)
    my_cap = lax.dynamic_slice_in_dim(bus_capacity, start, share_rows, 0)
    my_group = lax.dynamic_slice_in_dim(plant_group, start, share_rows, 0)
    by_group = jnp.take(irradiance_profile, my_group, axis=1)
    share = jnp.take(by_group, scenario_profile, axis=0).T
    upper = my_cap[:, None] * share
    lower = -my_load[:, None]
    base = my_inj - step_primal * my_cost[:, None]

    inject_half = injections.astype(jnp.bfloat16)
    by_place = shift_factors.reshape(YHI, XR, CORES, -1, shift_factors.shape[1])
    sf_keep = pick(by_place, core, 2)
    sf_send = pick(by_place, 1 - core, 2)

    def flow_part(x, mine):
        rows = pick(sf_keep if mine else sf_send, x, 1)
        return jnp.dot(rows, inject_half, preferred_element_type=jnp.float32)

    ring_out, outgoing_w = bus_reduce_scatter(flow_part, outgoing_w)
    arrived_w = lax.all_to_all(outgoing_w, "br", 0, 0, tiled=True)
    masked = jnp.where(block_hot[:, :, :, None], arrived_w[:, :, None, :], jnp.zeros((), jnp.bfloat16))
    masked = masked.reshape(slab_axis * CAP, YHI, XR, CORES, -1)
    masked_keep = pick(masked, core, 3)
    masked_send = pick(masked, 1 - core, 3)
    ring_out, masked_keep, masked_send, upper, lower, base = lax.optimization_barrier(
        (ring_out, masked_keep, masked_send, upper, lower, base)
    )
    flow = bus_pair_sum(ring_out)
    moved = prices + step_dual * flow
    bound = step_dual * limits[:, None]
    new_prices = moved - jnp.clip(moved, -bound, bound)
    price_half = new_prices.astype(jnp.bfloat16)
    prices_keep, prices_send = bus_all_gather(price_half)
    contract = (((0, 1, 2), (0, 1, 2)), ((), ()))
    partial_grad = lax.dot_general(sf_keep, prices_keep, contract, preferred_element_type=jnp.float32)
    partial_grad = partial_grad + lax.dot_general(sf_send, prices_send, contract, preferred_element_type=jnp.float32)
    contract_w = (((1, 2, 3), (0, 1, 2)), ((), ()))
    partial_rent = lax.dot_general(masked_keep, prices_keep, contract_w, preferred_element_type=jnp.float32)
    partial_rent = partial_rent + lax.dot_general(masked_send, prices_send, contract_w, preferred_element_type=jnp.float32)

    outgoing = jnp.concatenate(
        [partial_grad.reshape(slab_axis, share_rows, scenarios), partial_rent.reshape(slab_axis, CAP, scenarios)], axis=1
    )
    gathered = lax.all_to_all(outgoing, "br", 0, 0, tiled=True)
    gradient = jnp.sum(gathered[:, :share_rows], axis=0)
    returned = gathered[:, share_rows:]
    trial = base - step_primal * gradient
    my_new = jnp.minimum(jnp.maximum(trial, lower), upper)
    new_injections = lax.all_to_all(
        jnp.broadcast_to(my_new[None], (slab_axis, share_rows, scenarios)), "br", 0, 0, tiled=True
    ).reshape(bus_rows, scenarios)

    lookup = own_slab * CAP + own_slot
    fetched = jnp.take(returned.reshape(slab_axis * CAP, scenarios), lookup, axis=0)
    group_rent = jnp.sum(fetched.reshape(GDEV, list_len, scenarios), axis=1)
    return (new_injections, new_prices, group_rent)


def solution(mesh):
    placed = (
        P("br", "bus"),
        P("bus", None),
        P(("br", "bus"), None),
        P(("br", "bus")),
        P("bus"),
        P("bus"),
        P("bus"),
        P(),
        P("bus"),
        P(),
        P(),
        P(),
        P(("br", "bus"), None),
    )
    return jax.shard_map(
        per_device,
        mesh=mesh,
        in_specs=placed,
        out_specs=(P("bus", None), P(("br", "bus"), None), P(("br", "bus"), None)),
        check_vma=False,
    )
```

```python
import jax
import jax.numpy as jnp
from jax import lax
from jax.sharding import PartitionSpec as P

BLOCK = 512
CAP = 6
GDEV = 8


step_dual = 0.5
step_primal = 0.25


YHI, XR, CORES = 2, 4, 2


def bus_place():
    b = lax.axis_index("bus")
    return b // (XR * CORES), (b // CORES) % XR, b % CORES


def bus_perm(move):
    pairs = []
    for b in range(YHI * XR * CORES):
        yh, xi, c = b // (XR * CORES), (b // CORES) % XR, b % CORES
        ty, tx, tc = move(yh, xi, c)
        pairs.append((b, (ty * XR + tx) * CORES + tc))
    return pairs


CORE_SWAP = bus_perm(lambda y, x, c: (y, x, 1 - c))
X_UP = bus_perm(lambda y, x, c: (y, (x + 1) % XR, c))
X_DOWN = bus_perm(lambda y, x, c: (y, (x - 1) % XR, c))
Y_SWAP = bus_perm(lambda y, x, c: (1 - y, x, c))


def pick(a, i, axis):
    return lax.dynamic_index_in_dim(a, i, axis, keepdims=False)


def ring_scatter(contribs, up, rider=None):
    perm = X_UP if up else X_DOWN
    acc = contribs[0]
    for k, more in enumerate(contribs[1:]):
        acc = lax.ppermute(acc, "bus", perm) + more
        if k == 0 and rider is not None:
            acc, rider = lax.optimization_barrier((acc, rider))
    return acc, rider


def ring_gather(own, xi, up):
    step = 1 if up else -1
    perm = X_UP if up else X_DOWN
    out = jnp.zeros((XR,) + own.shape, own.dtype)
    cur = own
    for m in range(XR):
        if m:
            cur = lax.ppermute(cur, "bus", perm)
        out = lax.dynamic_update_index_in_dim(out, cur, (xi - step * m) % XR, 0)
    return out


def bus_reduce_scatter(flow_rows, inj, rider):
    yh, xi, c = bus_place()
    up, down, across = (xi + 1) % XR, (xi - 1) % XR, (xi + 2) % XR

    def exchanged(pieces, inj):
        return flow_rows(pieces, True, inj) + lax.ppermute(flow_rows(pieces, False, inj), "bus", CORE_SWAP)

    half = BLOCK // 2
    lead = [(down, 0, half), (up, half, half)]
    lead_send = flow_rows(lead, False, inj)
    lead_send, inj_second = lax.optimization_barrier((lead_send, inj))
    first = flow_rows(lead, True, inj) + lax.ppermute(lead_send, "bus", CORE_SWAP)
    second = exchanged([(across, 0, BLOCK)], inj_second)
    first, inj_rest = lax.optimization_barrier((first, inj))
    rest = exchanged([(up, 0, half), (down, half, half), (xi, 0, BLOCK)], inj_rest)
    cw, rider = ring_scatter(
        [first[:, :half], second[:, :half], rest[:, :half], rest[:, 2 * half:3 * half]], True, rider
    )
    ccw, _ = ring_scatter(
        [first[:, half:], second[:, half:], rest[:, half:2 * half], rest[:, 3 * half:]], False
    )
    z = jnp.concatenate([cw, ccw], axis=1)
    return z, rider


def bus_pair_sum(z):
    yh, xi, c = bus_place()
    return pick(z, yh, 0) + lax.ppermute(pick(z, 1 - yh, 0), "bus", Y_SWAP)


def bus_all_gather(p):
    yh, xi, c = bus_place()
    other = lax.ppermute(p, "bus", Y_SWAP)
    pair = jnp.where(yh == 0, jnp.stack([p, other]), jnp.stack([other, p]))
    half = p.shape[0] // 2
    cw = ring_gather(pair[:, :half], xi, True)
    ccw = ring_gather(pair[:, half:], xi, False)
    quad = jnp.moveaxis(jnp.concatenate([cw, ccw], axis=2), 0, 1)
    return quad, lax.ppermute(quad, "bus", CORE_SWAP)


def slots_of(slabs):
    positions = jnp.arange(slabs.shape[-1], dtype=jnp.int32)
    earlier = positions[None, :] < positions[:, None]
    same = slabs[..., :, None] == slabs[..., None, :]
    return jnp.sum((same & earlier).astype(jnp.int32), axis=-1)


def per_device(
    shift_factors,
    injections,
    prices,
    limits,
    unit_cost,
    bus_load,
    bus_capacity,
    irradiance_profile,
    plant_group,
    scenario_profile,
    listed_slab,
    listed_block,
    rent_weight,
):
    scenarios = injections.shape[1]
    bus_axis = lax.axis_size("bus")
    slab_axis = lax.axis_size("br")
    slab_index = lax.axis_index("br")
    column_index = lax.axis_index("bus")
    list_len = listed_slab.shape[1]
    entries = GDEV * list_len
    slab_rows = shift_factors.shape[0]
    blocks_per_slab = slab_rows // BLOCK

    slab_by_device = listed_slab.reshape(-1, entries)
    block_by_device = listed_block.reshape(-1, entries)
    self_device = slab_index * bus_axis + column_index
    own_slab = lax.dynamic_index_in_dim(slab_by_device, self_device, 0, keepdims=False)
    own_slot = slots_of(own_slab)
    slab_range = jnp.arange(slab_axis, dtype=jnp.int32)
    slot_range = jnp.arange(CAP, dtype=jnp.int32)
    pick_out = (own_slab[None, None, :] == slab_range[:, None, None]) & (
        own_slot[None, None, :] == slot_range[None, :, None]
    )
    weight_rows = rent_weight.reshape(entries, BLOCK)
    outgoing_w = jnp.einsum(
        "sce,er->scr", pick_out.astype(jnp.bfloat16), weight_rows, preferred_element_type=jnp.float32
    ).astype(jnp.bfloat16)
    sources = slab_range * bus_axis + column_index
    src_slab = jnp.take(slab_by_device, sources, axis=0)
    src_block = jnp.take(block_by_device, sources, axis=0)
    src_slot = slots_of(src_slab)
    pick_in = (src_slab[:, None, :] == slab_index) & (src_slot[:, None, :] == slot_range[None, :, None])
    block_choice = jnp.sum(jnp.where(pick_in, src_block[:, None, :], 0), axis=2)
    block_hot = block_choice[:, :, None] == jnp.arange(blocks_per_slab, dtype=jnp.int32)[None, None, :]
    yh, xi, core = bus_place()

    bus_rows = injections.shape[0]
    share_rows = bus_rows // slab_axis
    start = slab_index * share_rows
    my_inj = lax.dynamic_slice_in_dim(injections, start, share_rows, 0)
    my_cost = lax.dynamic_slice_in_dim(unit_cost, start, share_rows, 0)
    my_load = lax.dynamic_slice_in_dim(bus_load, start, share_rows, 0)
    my_cap = lax.dynamic_slice_in_dim(bus_capacity, start, share_rows, 0)
    my_group = lax.dynamic_slice_in_dim(plant_group, start, share_rows, 0)
    by_group = jnp.take(irradiance_profile, my_group, axis=1)
    share = jnp.take(by_group, scenario_profile, axis=0).T
    upper = my_cap[:, None] * share
    lower = -my_load[:, None]
    base = my_inj - step_primal * my_cost[:, None]

    inject_half = injections.astype(jnp.bfloat16)
    by_place = shift_factors.reshape(YHI, XR, CORES, -1, shift_factors.shape[1])
    sf_keep = pick(by_place, core, 2)
    sf_send = pick(by_place, 1 - core, 2)

    def flow_rows(pieces, mine, inj):
        own = sf_keep if mine else sf_send
        rows = [lax.dynamic_slice_in_dim(pick(own, x, 1), r0, n, 1) for x, r0, n in pieces]
        rows = rows[0] if len(rows) == 1 else jnp.concatenate(rows, axis=1)
        return jnp.dot(rows, inj, preferred_element_type=jnp.float32)

    ring_out, outgoing_w = bus_reduce_scatter(flow_rows, inject_half, outgoing_w)
    arrived_w = lax.all_to_all(outgoing_w, "br", 0, 0, tiled=True)
    masked = jnp.where(block_hot[:, :, :, None], arrived_w[:, :, None, :], jnp.zeros((), jnp.bfloat16))
    masked = masked.reshape(slab_axis * CAP, YHI, XR, CORES, -1)
    masked_keep = pick(masked, core, 3)
    masked_send = pick(masked, 1 - core, 3)
    ring_out, masked_keep, masked_send, upper, lower, base = lax.optimization_barrier(
        (ring_out, masked_keep, masked_send, upper, lower, base)
    )
    flow = bus_pair_sum(ring_out)
    moved = prices + step_dual * flow
    bound = step_dual * limits[:, None]
    new_prices = moved - jnp.clip(moved, -bound, bound)
    price_half = new_prices.astype(jnp.bfloat16)
    prices_keep, prices_send = bus_all_gather(price_half)
    contract = (((0, 1, 2), (0, 1, 2)), ((), ()))
    partial_grad = lax.dot_general(sf_keep, prices_keep, contract, preferred_element_type=jnp.float32)
    partial_grad = partial_grad + lax.dot_general(sf_send, prices_send, contract, preferred_element_type=jnp.float32)
    contract_w = (((1, 2, 3), (0, 1, 2)), ((), ()))
    partial_rent = lax.dot_general(masked_keep, prices_keep, contract_w, preferred_element_type=jnp.float32)
    partial_rent = partial_rent + lax.dot_general(masked_send, prices_send, contract_w, preferred_element_type=jnp.float32)

    outgoing = jnp.concatenate(
        [partial_grad.reshape(slab_axis, share_rows, scenarios), partial_rent.reshape(slab_axis, CAP, scenarios)], axis=1
    )
    gathered = lax.all_to_all(outgoing, "br", 0, 0, tiled=True)
    gradient = jnp.sum(gathered[:, :share_rows], axis=0)
    returned = gathered[:, share_rows:]
    trial = base - step_primal * gradient
    my_new = jnp.minimum(jnp.maximum(trial, lower), upper)
    new_injections = lax.all_to_all(
        jnp.broadcast_to(my_new[None], (slab_axis, share_rows, scenarios)), "br", 0, 0, tiled=True
    ).reshape(bus_rows, scenarios)

    lookup = own_slab * CAP + own_slot
    fetched = jnp.take(returned.reshape(slab_axis * CAP, scenarios), lookup, axis=0)
    group_rent = jnp.sum(fetched.reshape(GDEV, list_len, scenarios), axis=1)
    return (new_injections, new_prices, group_rent)


def solution(mesh):
    placed = (
        P("br", "bus"),
        P("bus", None),
        P(("br", "bus"), None),
        P(("br", "bus")),
        P("bus"),
        P("bus"),
        P("bus"),
        P(),
        P("bus"),
        P(),
        P(),
        P(),
        P(("br", "bus"), None),
    )
    return jax.shard_map(
        per_device,
        mesh=mesh,
        in_specs=placed,
        out_specs=(P("bus", None), P(("br", "bus"), None), P(("br", "bus"), None)),
        check_vma=False,
    )
```

```python
import jax
import jax.numpy as jnp
from jax import lax
from jax.sharding import PartitionSpec as P

BLOCK = 512
CAP = 6
GDEV = 8


step_dual = 0.5
step_primal = 0.25


YHI, XR, CORES = 2, 4, 2


def bus_place():
    b = lax.axis_index("bus")
    return b // (XR * CORES), (b // CORES) % XR, b % CORES


def bus_perm(move):
    pairs = []
    for b in range(YHI * XR * CORES):
        yh, xi, c = b // (XR * CORES), (b // CORES) % XR, b % CORES
        ty, tx, tc = move(yh, xi, c)
        pairs.append((b, (ty * XR + tx) * CORES + tc))
    return pairs


CORE_SWAP = bus_perm(lambda y, x, c: (y, x, 1 - c))
X_UP = bus_perm(lambda y, x, c: (y, (x + 1) % XR, c))
X_DOWN = bus_perm(lambda y, x, c: (y, (x - 1) % XR, c))
Y_SWAP = bus_perm(lambda y, x, c: (1 - y, x, c))


def pick(a, i, axis):
    return lax.dynamic_index_in_dim(a, i, axis, keepdims=False)


def ring_scatter(contribs, up, rider=None):
    perm = X_UP if up else X_DOWN
    acc = contribs[0]
    for k, more in enumerate(contribs[1:]):
        acc = lax.ppermute(acc, "bus", perm) + more
        if k == 0 and rider is not None:
            acc, rider = lax.optimization_barrier((acc, rider))
    return acc, rider


def ring_gather(own, xi, up):
    step = 1 if up else -1
    perm = X_UP if up else X_DOWN
    out = jnp.zeros((XR,) + own.shape, own.dtype)
    cur = own
    for m in range(XR):
        if m:
            cur = lax.ppermute(cur, "bus", perm)
        out = lax.dynamic_update_index_in_dim(out, cur, (xi - step * m) % XR, 0)
    return out


def bus_reduce_scatter(flow_part, rider):
    yh, xi, c = bus_place()
    first = [(xi - 1) % XR, (xi + 1) % XR]
    second = [(xi + 2) % XR, xi]
    summed = []
    for group in (first, second):
        send = flow_part(group, False)
        keep = flow_part(group, True)
        summed.append(keep + lax.ppermute(send, "bus", CORE_SWAP))
    a, b = summed
    half = a.shape[2] // 2
    cw, rider = ring_scatter([a[0, :, :half], b[0, :, :half], a[1, :, :half], b[1, :, :half]], True, rider)
    ccw, _ = ring_scatter([a[1, :, half:], b[0, :, half:], a[0, :, half:], b[1, :, half:]], False)
    z = jnp.concatenate([cw, ccw], axis=1)
    return z, rider


def bus_pair_sum(z):
    yh, xi, c = bus_place()
    return pick(z, yh, 0) + lax.ppermute(pick(z, 1 - yh, 0), "bus", Y_SWAP)


def bus_all_gather(p):
    yh, xi, c = bus_place()
    other = lax.ppermute(p, "bus", Y_SWAP)
    pair = jnp.where(yh == 0, jnp.stack([p, other]), jnp.stack([other, p]))
    half = p.shape[0] // 2
    cw = ring_gather(pair[:, :half], xi, True)
    ccw = ring_gather(pair[:, half:], xi, False)
    quad = jnp.moveaxis(jnp.concatenate([cw, ccw], axis=2), 0, 1)
    return quad, lax.ppermute(quad, "bus", CORE_SWAP)


def slots_of(slabs):
    positions = jnp.arange(slabs.shape[-1], dtype=jnp.int32)
    earlier = positions[None, :] < positions[:, None]
    same = slabs[..., :, None] == slabs[..., None, :]
    return jnp.sum((same & earlier).astype(jnp.int32), axis=-1)


def per_device(
    shift_factors,
    injections,
    prices,
    limits,
    unit_cost,
    bus_load,
    bus_capacity,
    irradiance_profile,
    plant_group,
    scenario_profile,
    listed_slab,
    listed_block,
    rent_weight,
):
    scenarios = injections.shape[1]
    bus_axis = lax.axis_size("bus")
    slab_axis = lax.axis_size("br")
    slab_index = lax.axis_index("br")
    column_index = lax.axis_index("bus")
    list_len = listed_slab.shape[1]
    entries = GDEV * list_len
    slab_rows = shift_factors.shape[0]
    blocks_per_slab = slab_rows // BLOCK

    slab_by_device = listed_slab.reshape(-1, entries)
    block_by_device = listed_block.reshape(-1, entries)
    self_device = slab_index * bus_axis + column_index
    own_slab = lax.dynamic_index_in_dim(slab_by_device, self_device, 0, keepdims=False)
    own_slot = slots_of(own_slab)
    slab_range = jnp.arange(slab_axis, dtype=jnp.int32)
    slot_range = jnp.arange(CAP, dtype=jnp.int32)
    pick_out = (own_slab[None, None, :] == slab_range[:, None, None]) & (
        own_slot[None, None, :] == slot_range[None, :, None]
    )
    weight_rows = rent_weight.reshape(entries, BLOCK)
    outgoing_w = jnp.einsum(
        "sce,er->scr", pick_out.astype(jnp.bfloat16), weight_rows, preferred_element_type=jnp.float32
    ).astype(jnp.bfloat16)
    yh, xi, core = bus_place()

    bus_rows = injections.shape[0]
    share_rows = bus_rows // slab_axis
    start = slab_index * share_rows
    inject_half = injections.astype(jnp.bfloat16)
    by_place = shift_factors.reshape(YHI, XR, CORES, -1, shift_factors.shape[1])
    sf_keep = pick(by_place, core, 2)
    sf_send = pick(by_place, 1 - core, 2)

    def flow_part(group, mine):
        rows = jnp.stack([pick(sf_keep if mine else sf_send, x, 1) for x in group])
        return jnp.dot(rows, inject_half, preferred_element_type=jnp.float32)

    rider = (outgoing_w, slab_by_device, block_by_device, irradiance_profile, plant_group, scenario_profile,
             unit_cost, bus_load, bus_capacity)
    ring_out, rider = bus_reduce_scatter(flow_part, rider)
    (outgoing_w, slab_by_device, block_by_device, irradiance_profile, plant_group, scenario_profile,
     unit_cost, bus_load, bus_capacity) = rider
    sources = slab_range * bus_axis + column_index
    src_slab = jnp.take(slab_by_device, sources, axis=0)
    src_block = jnp.take(block_by_device, sources, axis=0)
    src_slot = slots_of(src_slab)
    pick_in = (src_slab[:, None, :] == slab_index) & (src_slot[:, None, :] == slot_range[None, :, None])
    block_choice = jnp.sum(jnp.where(pick_in, src_block[:, None, :], 0), axis=2)
    block_hot = block_choice[:, :, None] == jnp.arange(blocks_per_slab, dtype=jnp.int32)[None, None, :]
    my_inj = lax.dynamic_slice_in_dim(injections, start, share_rows, 0)
    my_cost = lax.dynamic_slice_in_dim(unit_cost, start, share_rows, 0)
    my_load = lax.dynamic_slice_in_dim(bus_load, start, share_rows, 0)
    my_cap = lax.dynamic_slice_in_dim(bus_capacity, start, share_rows, 0)
    my_group = lax.dynamic_slice_in_dim(plant_group, start, share_rows, 0)
    by_group = jnp.take(irradiance_profile, my_group, axis=1)
    share = jnp.take(by_group, scenario_profile, axis=0).T
    upper = my_cap[:, None] * share
    lower = -my_load[:, None]
    base = my_inj - step_primal * my_cost[:, None]

    arrived_w = lax.all_to_all(outgoing_w, "br", 0, 0, tiled=True)
    masked = jnp.where(block_hot[:, :, :, None], arrived_w[:, :, None, :], jnp.zeros((), jnp.bfloat16))
    masked = masked.reshape(slab_axis * CAP, YHI, XR, CORES, -1)
    masked_keep = pick(masked, core, 3)
    masked_send = pick(masked, 1 - core, 3)
    ring_out, masked_keep, masked_send, upper, lower, base = lax.optimization_barrier(
        (ring_out, masked_keep, masked_send, upper, lower, base)
    )
    flow = bus_pair_sum(ring_out)
    moved = prices + step_dual * flow
    bound = step_dual * limits[:, None]
    new_prices = moved - jnp.clip(moved, -bound, bound)
    price_half = new_prices.astype(jnp.bfloat16)
    prices_keep, prices_send = bus_all_gather(price_half)
    contract = (((0, 1, 2), (0, 1, 2)), ((), ()))
    partial_grad = lax.dot_general(sf_keep, prices_keep, contract, preferred_element_type=jnp.float32)
    partial_grad = partial_grad + lax.dot_general(sf_send, prices_send, contract, preferred_element_type=jnp.float32)
    contract_w = (((1, 2, 3), (0, 1, 2)), ((), ()))
    partial_rent = lax.dot_general(masked_keep, prices_keep, contract_w, preferred_element_type=jnp.float32)
    partial_rent = partial_rent + lax.dot_general(masked_send, prices_send, contract_w, preferred_element_type=jnp.float32)

    outgoing = jnp.concatenate(
        [partial_grad.reshape(slab_axis, share_rows, scenarios), partial_rent.reshape(slab_axis, CAP, scenarios)], axis=1
    )
    gathered = lax.all_to_all(outgoing, "br", 0, 0, tiled=True)
    gradient = jnp.sum(gathered[:, :share_rows], axis=0)
    returned = gathered[:, share_rows:]
    trial = base - step_primal * gradient
    my_new = jnp.minimum(jnp.maximum(trial, lower), upper)
    new_injections = lax.all_to_all(
        jnp.broadcast_to(my_new[None], (slab_axis, share_rows, scenarios)), "br", 0, 0, tiled=True
    ).reshape(bus_rows, scenarios)

    lookup = own_slab * CAP + own_slot
    fetched = jnp.take(returned.reshape(slab_axis * CAP, scenarios), lookup, axis=0)
    group_rent = jnp.sum(fetched.reshape(GDEV, list_len, scenarios), axis=1)
    return (new_injections, new_prices, group_rent)


def solution(mesh):
    placed = (
        P("br", "bus"),
        P("bus", None),
        P(("br", "bus"), None),
        P(("br", "bus")),
        P("bus"),
        P("bus"),
        P("bus"),
        P(),
        P("bus"),
        P(),
        P(),
        P(),
        P(("br", "bus"), None),
    )
    return jax.shard_map(
        per_device,
        mesh=mesh,
        in_specs=placed,
        out_specs=(P("bus", None), P(("br", "bus"), None), P(("br", "bus"), None)),
        check_vma=False,
    )
```

```python
import jax
import jax.numpy as jnp
from jax import lax
from jax.sharding import PartitionSpec as P

BLOCK = 512
CAP = 6
GDEV = 8


step_dual = 0.5
step_primal = 0.25


YHI, XR, CORES = 2, 4, 2


def bus_place():
    b = lax.axis_index("bus")
    return b // (XR * CORES), (b // CORES) % XR, b % CORES


def bus_perm(move):
    pairs = []
    for b in range(YHI * XR * CORES):
        yh, xi, c = b // (XR * CORES), (b // CORES) % XR, b % CORES
        ty, tx, tc = move(yh, xi, c)
        pairs.append((b, (ty * XR + tx) * CORES + tc))
    return pairs


CORE_SWAP = bus_perm(lambda y, x, c: (y, x, 1 - c))
X_UP = bus_perm(lambda y, x, c: (y, (x + 1) % XR, c))
X_DOWN = bus_perm(lambda y, x, c: (y, (x - 1) % XR, c))
Y_SWAP = bus_perm(lambda y, x, c: (1 - y, x, c))


def pick(a, i, axis):
    return lax.dynamic_index_in_dim(a, i, axis, keepdims=False)


def ring_scatter(contribs, up, rider=None):
    perm = X_UP if up else X_DOWN
    acc = contribs[0]
    for k, more in enumerate(contribs[1:]):
        acc = lax.ppermute(acc, "bus", perm) + more
        if k == 0 and rider is not None:
            acc, rider = lax.optimization_barrier((acc, rider))
    return acc, rider


def ring_gather(own, xi, up):
    step = 1 if up else -1
    perm = X_UP if up else X_DOWN
    out = jnp.zeros((XR,) + own.shape, own.dtype)
    cur = own
    for m in range(XR):
        if m:
            cur = lax.ppermute(cur, "bus", perm)
        out = lax.dynamic_update_index_in_dim(out, cur, (xi - step * m) % XR, 0)
    return out


def bus_reduce_scatter(flow_part, rider):
    yh, xi, c = bus_place()
    first = [(xi - 1) % XR, (xi + 1) % XR]
    second = [(xi + 2) % XR, xi]
    summed = []
    for group in (first, second):
        send = jnp.stack([flow_part(x, False) for x in group])
        keep = jnp.stack([flow_part(x, True) for x in group])
        summed.append(keep + lax.ppermute(send, "bus", CORE_SWAP))
    a, b = summed
    half = a.shape[2] // 2
    cw, rider = ring_scatter([a[0, :, :half], b[0, :, :half], a[1, :, :half], b[1, :, :half]], True, rider)
    ccw, _ = ring_scatter([a[1, :, half:], b[0, :, half:], a[0, :, half:], b[1, :, half:]], False)
    z = jnp.concatenate([cw, ccw], axis=1)
    return z, rider


def bus_pair_sum(z):
    yh, xi, c = bus_place()
    return pick(z, yh, 0) + lax.ppermute(pick(z, 1 - yh, 0), "bus", Y_SWAP)


def bus_all_gather(p):
    yh, xi, c = bus_place()
    other = lax.ppermute(p, "bus", Y_SWAP)
    pair = jnp.where(yh == 0, jnp.stack([p, other]), jnp.stack([other, p]))
    half = p.shape[0] // 2
    cw = ring_gather(pair[:, :half], xi, True)
    ccw = ring_gather(pair[:, half:], xi, False)
    quad = jnp.moveaxis(jnp.concatenate([cw, ccw], axis=2), 0, 1)
    return quad, lax.ppermute(quad, "bus", CORE_SWAP)


def slots_of(slabs):
    positions = jnp.arange(slabs.shape[-1], dtype=jnp.int32)
    earlier = positions[None, :] < positions[:, None]
    same = slabs[..., :, None] == slabs[..., None, :]
    return jnp.sum((same & earlier).astype(jnp.int32), axis=-1)


def per_device(
    shift_factors,
    injections,
    prices,
    limits,
    unit_cost,
    bus_load,
    bus_capacity,
    irradiance_profile,
    plant_group,
    scenario_profile,
    listed_slab,
    listed_block,
    rent_weight,
):
    scenarios = injections.shape[1]
    bus_axis = lax.axis_size("bus")
    slab_axis = lax.axis_size("br")
    slab_index = lax.axis_index("br")
    column_index = lax.axis_index("bus")
    list_len = listed_slab.shape[1]
    entries = GDEV * list_len
    slab_rows = shift_factors.shape[0]
    blocks_per_slab = slab_rows // BLOCK

    slab_by_device = listed_slab.reshape(-1, entries)
    block_by_device = listed_block.reshape(-1, entries)
    self_device = slab_index * bus_axis + column_index
    own_slab = lax.dynamic_index_in_dim(slab_by_device, self_device, 0, keepdims=False)
    own_slot = slots_of(own_slab)
    slab_range = jnp.arange(slab_axis, dtype=jnp.int32)
    slot_range = jnp.arange(CAP, dtype=jnp.int32)
    pick_out = (own_slab[None, None, :] == slab_range[:, None, None]) & (
        own_slot[None, None, :] == slot_range[None, :, None]
    )
    weight_rows = rent_weight.reshape(entries, BLOCK)
    outgoing_w = jnp.einsum(
        "sce,er->scr", pick_out.astype(jnp.bfloat16), weight_rows, preferred_element_type=jnp.float32
    ).astype(jnp.bfloat16)
    sources = slab_range * bus_axis + column_index
    src_slab = jnp.take(slab_by_device, sources, axis=0)
    src_block = jnp.take(block_by_device, sources, axis=0)
    src_slot = slots_of(src_slab)
    pick_in = (src_slab[:, None, :] == slab_index) & (src_slot[:, None, :] == slot_range[None, :, None])
    block_choice = jnp.sum(jnp.where(pick_in, src_block[:, None, :], 0), axis=2)
    block_hot = block_choice[:, :, None] == jnp.arange(blocks_per_slab, dtype=jnp.int32)[None, None, :]
    yh, xi, core = bus_place()

    bus_rows = injections.shape[0]
    share_rows = bus_rows // slab_axis
    start = slab_index * share_rows
    my_inj = lax.dynamic_slice_in_dim(injections, start, share_rows, 0)
    my_cost = lax.dynamic_slice_in_dim(unit_cost, start, share_rows, 0)
    my_load = lax.dynamic_slice_in_dim(bus_load, start, share_rows, 0)
    my_cap = lax.dynamic_slice_in_dim(bus_capacity, start, share_rows, 0)
    my_group = lax.dynamic_slice_in_dim(plant_group, start, share_rows, 0)
    by_group = jnp.take(irradiance_profile, my_group, axis=1)
    share = jnp.take(by_group, scenario_profile, axis=0).T
    upper = my_cap[:, None] * share
    lower = -my_load[:, None]
    base = my_inj - step_primal * my_cost[:, None]

    inject_half = injections.astype(jnp.bfloat16)
    by_place = shift_factors.reshape(YHI, XR, CORES, -1, shift_factors.shape[1])
    sf_keep = pick(by_place, core, 2)
    sf_send = pick(by_place, 1 - core, 2)

    def flow_part(x, mine):
        rows = pick(sf_keep if mine else sf_send, x, 1)
        return jnp.dot(rows, inject_half, preferred_element_type=jnp.float32)

    ring_out, outgoing_w = bus_reduce_scatter(flow_part, outgoing_w)
    arrived_w = lax.all_to_all(outgoing_w, "br", 0, 0, tiled=True)
    masked = jnp.where(block_hot[:, :, :, None], arrived_w[:, :, None, :], jnp.zeros((), jnp.bfloat16))
    masked = masked.reshape(slab_axis * CAP, YHI, XR, CORES, -1)
    masked_keep = pick(masked, core, 3)
    masked_send = pick(masked, 1 - core, 3)
    ring_out, upper, lower, base = lax.optimization_barrier((ring_out, upper, lower, base))
    flow = bus_pair_sum(ring_out)
    flow, masked_keep, masked_send = lax.optimization_barrier((flow, masked_keep, masked_send))
    moved = prices + step_dual * flow
    bound = step_dual * limits[:, None]
    new_prices = moved - jnp.clip(moved, -bound, bound)
    price_half = new_prices.astype(jnp.bfloat16)
    prices_keep, prices_send = bus_all_gather(price_half)
    contract = (((0, 1, 2), (0, 1, 2)), ((), ()))
    partial_grad = lax.dot_general(sf_keep, prices_keep, contract, preferred_element_type=jnp.float32)
    partial_grad = partial_grad + lax.dot_general(sf_send, prices_send, contract, preferred_element_type=jnp.float32)
    contract_w = (((1, 2, 3), (0, 1, 2)), ((), ()))
    partial_rent = lax.dot_general(masked_keep, prices_keep, contract_w, preferred_element_type=jnp.float32)
    partial_rent = partial_rent + lax.dot_general(masked_send, prices_send, contract_w, preferred_element_type=jnp.float32)

    outgoing = jnp.concatenate(
        [partial_grad.reshape(slab_axis, share_rows, scenarios), partial_rent.reshape(slab_axis, CAP, scenarios)], axis=1
    )
    gathered = lax.all_to_all(outgoing, "br", 0, 0, tiled=True)
    gradient = jnp.sum(gathered[:, :share_rows], axis=0)
    returned = gathered[:, share_rows:]
    trial = base - step_primal * gradient
    my_new = jnp.minimum(jnp.maximum(trial, lower), upper)
    new_injections = lax.all_to_all(
        jnp.broadcast_to(my_new[None], (slab_axis, share_rows, scenarios)), "br", 0, 0, tiled=True
    ).reshape(bus_rows, scenarios)

    lookup = own_slab * CAP + own_slot
    fetched = jnp.take(returned.reshape(slab_axis * CAP, scenarios), lookup, axis=0)
    group_rent = jnp.sum(fetched.reshape(GDEV, list_len, scenarios), axis=1)
    return (new_injections, new_prices, group_rent)


def solution(mesh):
    placed = (
        P("br", "bus"),
        P("bus", None),
        P(("br", "bus"), None),
        P(("br", "bus")),
        P("bus"),
        P("bus"),
        P("bus"),
        P(),
        P("bus"),
        P(),
        P(),
        P(),
        P(("br", "bus"), None),
    )
    return jax.shard_map(
        per_device,
        mesh=mesh,
        in_specs=placed,
        out_specs=(P("bus", None), P(("br", "bus"), None), P(("br", "bus"), None)),
        check_vma=False,
    )
```

```python
import jax
import jax.numpy as jnp
from jax import lax
from jax.sharding import PartitionSpec as P

BLOCK = 512
CAP = 6
GDEV = 8


step_dual = 0.5
step_primal = 0.25


YHI, XR, CORES = 2, 4, 2


def bus_place():
    b = lax.axis_index("bus")
    return b // (XR * CORES), (b // CORES) % XR, b % CORES


def bus_perm(move):
    pairs = []
    for b in range(YHI * XR * CORES):
        yh, xi, c = b // (XR * CORES), (b // CORES) % XR, b % CORES
        ty, tx, tc = move(yh, xi, c)
        pairs.append((b, (ty * XR + tx) * CORES + tc))
    return pairs


CORE_SWAP = bus_perm(lambda y, x, c: (y, x, 1 - c))
X_UP = bus_perm(lambda y, x, c: (y, (x + 1) % XR, c))
X_DOWN = bus_perm(lambda y, x, c: (y, (x - 1) % XR, c))
Y_SWAP = bus_perm(lambda y, x, c: (1 - y, x, c))


def pick(a, i, axis):
    return lax.dynamic_index_in_dim(a, i, axis, keepdims=False)


def ring_scatter(contribs, up, rider=None):
    perm = X_UP if up else X_DOWN
    acc = contribs[0]
    for k, more in enumerate(contribs[1:]):
        acc = lax.ppermute(acc, "bus", perm) + more
        if k == 0 and rider is not None:
            acc, rider = lax.optimization_barrier((acc, rider))
    return acc, rider


def ring_gather(own, xi, up):
    step = 1 if up else -1
    perm = X_UP if up else X_DOWN
    out = jnp.zeros((XR,) + own.shape, own.dtype)
    cur = own
    for m in range(XR):
        if m:
            cur = lax.ppermute(cur, "bus", perm)
        out = lax.dynamic_update_index_in_dim(out, cur, (xi - step * m) % XR, 0)
    return out


def bus_reduce_scatter(flow_part, rider):
    yh, xi, c = bus_place()
    first = [(xi - 1) % XR, (xi + 1) % XR]
    second = [(xi + 2) % XR, xi]
    summed = []
    for group in (first, second):
        send = jnp.stack([flow_part(x, False) for x in group])
        keep = jnp.stack([flow_part(x, True) for x in group])
        summed.append(keep + lax.ppermute(send, "bus", CORE_SWAP))
    a, b = summed
    q = a.shape[2] // 4
    half = 2 * q
    cw, rider = ring_scatter([a[0, :, :q], b[0, :, :q], a[1, :, :q], b[1, :, :q]], True, rider)
    ccw, _ = ring_scatter([a[1, :, q:half], b[0, :, q:half], a[0, :, q:half], b[1, :, q:half]], False)
    late = jnp.concatenate([a[:, :, half:], b[:, :, half:]], axis=0)
    late = pick(late, yh, 1) + lax.ppermute(pick(late, 1 - yh, 1), "bus", Y_SWAP)
    cw_late, _ = ring_scatter([late[0, :q], late[2, :q], late[1, :q], late[3, :q]], True)
    ccw_late, _ = ring_scatter([late[1, q:], late[2, q:], late[0, q:], late[3, q:]], False)
    early = bus_pair_sum(jnp.concatenate([cw, ccw], axis=1))
    return jnp.concatenate([early, cw_late, ccw_late], axis=0), rider


def bus_pair_sum(z):
    yh, xi, c = bus_place()
    return pick(z, yh, 0) + lax.ppermute(pick(z, 1 - yh, 0), "bus", Y_SWAP)


def bus_all_gather(p):
    yh, xi, c = bus_place()
    other = lax.ppermute(p, "bus", Y_SWAP)
    pair = jnp.where(yh == 0, jnp.stack([p, other]), jnp.stack([other, p]))
    half = p.shape[0] // 2
    cw = ring_gather(pair[:, :half], xi, True)
    ccw = ring_gather(pair[:, half:], xi, False)
    quad = jnp.moveaxis(jnp.concatenate([cw, ccw], axis=2), 0, 1)
    return quad, lax.ppermute(quad, "bus", CORE_SWAP)


def slots_of(slabs):
    positions = jnp.arange(slabs.shape[-1], dtype=jnp.int32)
    earlier = positions[None, :] < positions[:, None]
    same = slabs[..., :, None] == slabs[..., None, :]
    return jnp.sum((same & earlier).astype(jnp.int32), axis=-1)


def per_device(
    shift_factors,
    injections,
    prices,
    limits,
    unit_cost,
    bus_load,
    bus_capacity,
    irradiance_profile,
    plant_group,
    scenario_profile,
    listed_slab,
    listed_block,
    rent_weight,
):
    scenarios = injections.shape[1]
    bus_axis = lax.axis_size("bus")
    slab_axis = lax.axis_size("br")
    slab_index = lax.axis_index("br")
    column_index = lax.axis_index("bus")
    list_len = listed_slab.shape[1]
    entries = GDEV * list_len
    slab_rows = shift_factors.shape[0]
    blocks_per_slab = slab_rows // BLOCK

    slab_by_device = listed_slab.reshape(-1, entries)
    block_by_device = listed_block.reshape(-1, entries)
    self_device = slab_index * bus_axis + column_index
    own_slab = lax.dynamic_index_in_dim(slab_by_device, self_device, 0, keepdims=False)
    own_slot = slots_of(own_slab)
    slab_range = jnp.arange(slab_axis, dtype=jnp.int32)
    slot_range = jnp.arange(CAP, dtype=jnp.int32)
    pick_out = (own_slab[None, None, :] == slab_range[:, None, None]) & (
        own_slot[None, None, :] == slot_range[None, :, None]
    )
    weight_rows = rent_weight.reshape(entries, BLOCK)
    outgoing_w = jnp.einsum(
        "sce,er->scr", pick_out.astype(jnp.bfloat16), weight_rows, preferred_element_type=jnp.float32
    ).astype(jnp.bfloat16)
    sources = slab_range * bus_axis + column_index
    src_slab = jnp.take(slab_by_device, sources, axis=0)
    src_block = jnp.take(block_by_device, sources, axis=0)
    src_slot = slots_of(src_slab)
    pick_in = (src_slab[:, None, :] == slab_index) & (src_slot[:, None, :] == slot_range[None, :, None])
    block_choice = jnp.sum(jnp.where(pick_in, src_block[:, None, :], 0), axis=2)
    block_hot = block_choice[:, :, None] == jnp.arange(blocks_per_slab, dtype=jnp.int32)[None, None, :]
    yh, xi, core = bus_place()

    bus_rows = injections.shape[0]
    share_rows = bus_rows // slab_axis
    start = slab_index * share_rows
    my_inj = lax.dynamic_slice_in_dim(injections, start, share_rows, 0)
    my_cost = lax.dynamic_slice_in_dim(unit_cost, start, share_rows, 0)
    my_load = lax.dynamic_slice_in_dim(bus_load, start, share_rows, 0)
    my_cap = lax.dynamic_slice_in_dim(bus_capacity, start, share_rows, 0)
    my_group = lax.dynamic_slice_in_dim(plant_group, start, share_rows, 0)
    by_group = jnp.take(irradiance_profile, my_group, axis=1)
    share = jnp.take(by_group, scenario_profile, axis=0).T
    upper = my_cap[:, None] * share
    lower = -my_load[:, None]
    base = my_inj - step_primal * my_cost[:, None]

    inject_half = injections.astype(jnp.bfloat16)
    by_place = shift_factors.reshape(YHI, XR, CORES, -1, shift_factors.shape[1])
    sf_keep = pick(by_place, core, 2)
    sf_send = pick(by_place, 1 - core, 2)

    def flow_part(x, mine):
        rows = pick(sf_keep if mine else sf_send, x, 1)
        return jnp.dot(rows, inject_half, preferred_element_type=jnp.float32)

    ring_out, outgoing_w = bus_reduce_scatter(flow_part, outgoing_w)
    arrived_w = lax.all_to_all(outgoing_w, "br", 0, 0, tiled=True)
    masked = jnp.where(block_hot[:, :, :, None], arrived_w[:, :, None, :], jnp.zeros((), jnp.bfloat16))
    masked = masked.reshape(slab_axis * CAP, YHI, XR, CORES, -1)
    masked_keep = pick(masked, core, 3)
    masked_send = pick(masked, 1 - core, 3)
    flow, masked_keep, masked_send, upper, lower, base = lax.optimization_barrier(
        (ring_out, masked_keep, masked_send, upper, lower, base)
    )
    moved = prices + step_dual * flow
    bound = step_dual * limits[:, None]
    new_prices = moved - jnp.clip(moved, -bound, bound)
    price_half = new_prices.astype(jnp.bfloat16)
    prices_keep, prices_send = bus_all_gather(price_half)
    contract = (((0, 1, 2), (0, 1, 2)), ((), ()))
    partial_grad = lax.dot_general(sf_keep, prices_keep, contract, preferred_element_type=jnp.float32)
    partial_grad = partial_grad + lax.dot_general(sf_send, prices_send, contract, preferred_element_type=jnp.float32)
    contract_w = (((1, 2, 3), (0, 1, 2)), ((), ()))
    partial_rent = lax.dot_general(masked_keep, prices_keep, contract_w, preferred_element_type=jnp.float32)
    partial_rent = partial_rent + lax.dot_general(masked_send, prices_send, contract_w, preferred_element_type=jnp.float32)

    outgoing = jnp.concatenate(
        [partial_grad.reshape(slab_axis, share_rows, scenarios), partial_rent.reshape(slab_axis, CAP, scenarios)], axis=1
    )
    gathered = lax.all_to_all(outgoing, "br", 0, 0, tiled=True)
    gradient = jnp.sum(gathered[:, :share_rows], axis=0)
    returned = gathered[:, share_rows:]
    trial = base - step_primal * gradient
    my_new = jnp.minimum(jnp.maximum(trial, lower), upper)
    new_injections = lax.all_to_all(
        jnp.broadcast_to(my_new[None], (slab_axis, share_rows, scenarios)), "br", 0, 0, tiled=True
    ).reshape(bus_rows, scenarios)

    lookup = own_slab * CAP + own_slot
    fetched = jnp.take(returned.reshape(slab_axis * CAP, scenarios), lookup, axis=0)
    group_rent = jnp.sum(fetched.reshape(GDEV, list_len, scenarios), axis=1)
    return (new_injections, new_prices, group_rent)


def solution(mesh):
    placed = (
        P("br", "bus"),
        P("bus", None),
        P(("br", "bus"), None),
        P(("br", "bus")),
        P("bus"),
        P("bus"),
        P("bus"),
        P(),
        P("bus"),
        P(),
        P(),
        P(),
        P(("br", "bus"), None),
    )
    return jax.shard_map(
        per_device,
        mesh=mesh,
        in_specs=placed,
        out_specs=(P("bus", None), P(("br", "bus"), None), P(("br", "bus"), None)),
        check_vma=False,
    )
```

```python
import jax
import jax.numpy as jnp
from jax import lax
from jax.sharding import PartitionSpec as P

BLOCK = 512
CAP = 6
GDEV = 8


step_dual = 0.5
step_primal = 0.25


YHI, XR, CORES = 2, 4, 2


def bus_place():
    b = lax.axis_index("bus")
    return b // (XR * CORES), (b // CORES) % XR, b % CORES


def bus_perm(move):
    pairs = []
    for b in range(YHI * XR * CORES):
        yh, xi, c = b // (XR * CORES), (b // CORES) % XR, b % CORES
        ty, tx, tc = move(yh, xi, c)
        pairs.append((b, (ty * XR + tx) * CORES + tc))
    return pairs


CORE_SWAP = bus_perm(lambda y, x, c: (y, x, 1 - c))
X_UP = bus_perm(lambda y, x, c: (y, (x + 1) % XR, c))
X_DOWN = bus_perm(lambda y, x, c: (y, (x - 1) % XR, c))
Y_SWAP = bus_perm(lambda y, x, c: (1 - y, x, c))


def pick(a, i, axis):
    return lax.dynamic_index_in_dim(a, i, axis, keepdims=False)


def ring_scatter(contribs, up, rider=None):
    perm = X_UP if up else X_DOWN
    acc = contribs[0]
    for k, more in enumerate(contribs[1:]):
        acc = lax.ppermute(acc, "bus", perm) + more
        if k == 1 and rider is not None:
            acc, rider = lax.optimization_barrier((acc, rider))
    return acc, rider


def ring_gather(own, xi, up):
    step = 1 if up else -1
    perm = X_UP if up else X_DOWN
    out = jnp.zeros((XR,) + own.shape, own.dtype)
    cur = own
    for m in range(XR):
        if m:
            cur = lax.ppermute(cur, "bus", perm)
        out = lax.dynamic_update_index_in_dim(out, cur, (xi - step * m) % XR, 0)
    return out


def bus_reduce_scatter(flow_part, rider):
    yh, xi, c = bus_place()
    first = [(xi - 1) % XR, (xi + 1) % XR]
    second = [(xi + 2) % XR, xi]
    summed = []
    for group in (first, second):
        send = jnp.stack([flow_part(x, False) for x in group])
        keep = jnp.stack([flow_part(x, True) for x in group])
        summed.append(keep + lax.ppermute(send, "bus", CORE_SWAP))
    a, b = summed
    q = a.shape[2] // 4
    half = 2 * q
    cw, rider = ring_scatter([a[0, :, :q], b[0, :, :q], a[1, :, :q], b[1, :, :q]], True, rider)
    ccw, _ = ring_scatter([a[1, :, q:half], b[0, :, q:half], a[0, :, q:half], b[1, :, q:half]], False)
    late = jnp.concatenate([a[:, :, half:], b[:, :, half:]], axis=0)
    late = pick(late, yh, 1) + lax.ppermute(pick(late, 1 - yh, 1), "bus", Y_SWAP)
    cw_late, _ = ring_scatter([late[0, :q], late[2, :q], late[1, :q], late[3, :q]], True)
    ccw_late, _ = ring_scatter([late[1, q:], late[2, q:], late[0, q:], late[3, q:]], False)
    early = bus_pair_sum(jnp.concatenate([cw, ccw], axis=1))
    return jnp.concatenate([early, cw_late, ccw_late], axis=0), rider


def bus_pair_sum(z):
    yh, xi, c = bus_place()
    return pick(z, yh, 0) + lax.ppermute(pick(z, 1 - yh, 0), "bus", Y_SWAP)


def bus_all_gather(p):
    yh, xi, c = bus_place()
    other = lax.ppermute(p, "bus", Y_SWAP)
    pair = jnp.where(yh == 0, jnp.stack([p, other]), jnp.stack([other, p]))
    half = p.shape[0] // 2
    cw = ring_gather(pair[:, :half], xi, True)
    ccw = ring_gather(pair[:, half:], xi, False)
    quad = jnp.moveaxis(jnp.concatenate([cw, ccw], axis=2), 0, 1)
    return quad, lax.ppermute(quad, "bus", CORE_SWAP)


def slots_of(slabs):
    positions = jnp.arange(slabs.shape[-1], dtype=jnp.int32)
    earlier = positions[None, :] < positions[:, None]
    same = slabs[..., :, None] == slabs[..., None, :]
    return jnp.sum((same & earlier).astype(jnp.int32), axis=-1)


def per_device(
    shift_factors,
    injections,
    prices,
    limits,
    unit_cost,
    bus_load,
    bus_capacity,
    irradiance_profile,
    plant_group,
    scenario_profile,
    listed_slab,
    listed_block,
    rent_weight,
):
    scenarios = injections.shape[1]
    bus_axis = lax.axis_size("bus")
    slab_axis = lax.axis_size("br")
    slab_index = lax.axis_index("br")
    column_index = lax.axis_index("bus")
    list_len = listed_slab.shape[1]
    entries = GDEV * list_len
    slab_rows = shift_factors.shape[0]
    blocks_per_slab = slab_rows // BLOCK

    slab_by_device = listed_slab.reshape(-1, entries)
    block_by_device = listed_block.reshape(-1, entries)
    self_device = slab_index * bus_axis + column_index
    own_slab = lax.dynamic_index_in_dim(slab_by_device, self_device, 0, keepdims=False)
    own_slot = slots_of(own_slab)
    slab_range = jnp.arange(slab_axis, dtype=jnp.int32)
    slot_range = jnp.arange(CAP, dtype=jnp.int32)
    pick_out = (own_slab[None, None, :] == slab_range[:, None, None]) & (
        own_slot[None, None, :] == slot_range[None, :, None]
    )
    weight_rows = rent_weight.reshape(entries, BLOCK)
    outgoing_w = jnp.einsum(
        "sce,er->scr", pick_out.astype(jnp.bfloat16), weight_rows, preferred_element_type=jnp.float32
    ).astype(jnp.bfloat16)
    sources = slab_range * bus_axis + column_index
    src_slab = jnp.take(slab_by_device, sources, axis=0)
    src_block = jnp.take(block_by_device, sources, axis=0)
    src_slot = slots_of(src_slab)
    pick_in = (src_slab[:, None, :] == slab_index) & (src_slot[:, None, :] == slot_range[None, :, None])
    block_choice = jnp.sum(jnp.where(pick_in, src_block[:, None, :], 0), axis=2)
    block_hot = block_choice[:, :, None] == jnp.arange(blocks_per_slab, dtype=jnp.int32)[None, None, :]
    yh, xi, core = bus_place()

    bus_rows = injections.shape[0]
    share_rows = bus_rows // slab_axis
    start = slab_index * share_rows
    my_inj = lax.dynamic_slice_in_dim(injections, start, share_rows, 0)
    my_cost = lax.dynamic_slice_in_dim(unit_cost, start, share_rows, 0)
    my_load = lax.dynamic_slice_in_dim(bus_load, start, share_rows, 0)
    my_cap = lax.dynamic_slice_in_dim(bus_capacity, start, share_rows, 0)
    my_group = lax.dynamic_slice_in_dim(plant_group, start, share_rows, 0)
    by_group = jnp.take(irradiance_profile, my_group, axis=1)
    share = jnp.take(by_group, scenario_profile, axis=0).T
    upper = my_cap[:, None] * share
    lower = -my_load[:, None]
    base = my_inj - step_primal * my_cost[:, None]

    inject_half = injections.astype(jnp.bfloat16)
    by_place = shift_factors.reshape(YHI, XR, CORES, -1, shift_factors.shape[1])
    sf_keep = pick(by_place, core, 2)
    sf_send = pick(by_place, 1 - core, 2)

    def flow_part(x, mine):
        rows = pick(sf_keep if mine else sf_send, x, 1)
        return jnp.dot(rows, inject_half, preferred_element_type=jnp.float32)

    ring_out, outgoing_w = bus_reduce_scatter(flow_part, outgoing_w)
    arrived_w = lax.all_to_all(outgoing_w, "br", 0, 0, tiled=True)
    masked = jnp.where(block_hot[:, :, :, None], arrived_w[:, :, None, :], jnp.zeros((), jnp.bfloat16))
    masked = masked.reshape(slab_axis * CAP, YHI, XR, CORES, -1)
    masked_keep = pick(masked, core, 3)
    masked_send = pick(masked, 1 - core, 3)
    flow, masked_keep, masked_send, upper, lower, base = lax.optimization_barrier(
        (ring_out, masked_keep, masked_send, upper, lower, base)
    )
    moved = prices + step_dual * flow
    bound = step_dual * limits[:, None]
    new_prices = moved - jnp.clip(moved, -bound, bound)
    price_half = new_prices.astype(jnp.bfloat16)
    prices_keep, prices_send = bus_all_gather(price_half)
    contract = (((0, 1, 2), (0, 1, 2)), ((), ()))
    partial_grad = lax.dot_general(sf_keep, prices_keep, contract, preferred_element_type=jnp.float32)
    partial_grad = partial_grad + lax.dot_general(sf_send, prices_send, contract, preferred_element_type=jnp.float32)
    contract_w = (((1, 2, 3), (0, 1, 2)), ((), ()))
    partial_rent = lax.dot_general(masked_keep, prices_keep, contract_w, preferred_element_type=jnp.float32)
    partial_rent = partial_rent + lax.dot_general(masked_send, prices_send, contract_w, preferred_element_type=jnp.float32)

    outgoing = jnp.concatenate(
        [partial_grad.reshape(slab_axis, share_rows, scenarios), partial_rent.reshape(slab_axis, CAP, scenarios)], axis=1
    )
    gathered = lax.all_to_all(outgoing, "br", 0, 0, tiled=True)
    gradient = jnp.sum(gathered[:, :share_rows], axis=0)
    returned = gathered[:, share_rows:]
    trial = base - step_primal * gradient
    my_new = jnp.minimum(jnp.maximum(trial, lower), upper)
    new_injections = lax.all_to_all(
        jnp.broadcast_to(my_new[None], (slab_axis, share_rows, scenarios)), "br", 0, 0, tiled=True
    ).reshape(bus_rows, scenarios)

    lookup = own_slab * CAP + own_slot
    fetched = jnp.take(returned.reshape(slab_axis * CAP, scenarios), lookup, axis=0)
    group_rent = jnp.sum(fetched.reshape(GDEV, list_len, scenarios), axis=1)
    return (new_injections, new_prices, group_rent)


def solution(mesh):
    placed = (
        P("br", "bus"),
        P("bus", None),
        P(("br", "bus"), None),
        P(("br", "bus")),
        P("bus"),
        P("bus"),
        P("bus"),
        P(),
        P("bus"),
        P(),
        P(),
        P(),
        P(("br", "bus"), None),
    )
    return jax.shard_map(
        per_device,
        mesh=mesh,
        in_specs=placed,
        out_specs=(P("bus", None), P(("br", "bus"), None), P(("br", "bus"), None)),
        check_vma=False,
    )
```

```python
import jax
import jax.numpy as jnp
from jax import lax
from jax.sharding import PartitionSpec as P

BLOCK = 512
CAP = 6
GDEV = 8


step_dual = 0.5
step_primal = 0.25


YHI, XR, CORES = 2, 4, 2


def bus_place():
    b = lax.axis_index("bus")
    return b // (XR * CORES), (b // CORES) % XR, b % CORES


def bus_perm(move):
    pairs = []
    for b in range(YHI * XR * CORES):
        yh, xi, c = b // (XR * CORES), (b // CORES) % XR, b % CORES
        ty, tx, tc = move(yh, xi, c)
        pairs.append((b, (ty * XR + tx) * CORES + tc))
    return pairs


CORE_SWAP = bus_perm(lambda y, x, c: (y, x, 1 - c))
X_UP = bus_perm(lambda y, x, c: (y, (x + 1) % XR, c))
X_DOWN = bus_perm(lambda y, x, c: (y, (x - 1) % XR, c))
Y_SWAP = bus_perm(lambda y, x, c: (1 - y, x, c))


def pick(a, i, axis):
    return lax.dynamic_index_in_dim(a, i, axis, keepdims=False)


def ring_scatter(contribs, up, rider=None):
    perm = X_UP if up else X_DOWN
    acc = contribs[0]
    for k, more in enumerate(contribs[1:]):
        acc = lax.ppermute(acc, "bus", perm) + more
        if k == 0 and rider is not None:
            acc, rider = lax.optimization_barrier((acc, rider))
    return acc, rider


def ring_gather(own, xi, up):
    step = 1 if up else -1
    perm = X_UP if up else X_DOWN
    out = jnp.zeros((XR,) + own.shape, own.dtype)
    cur = own
    for m in range(XR):
        if m:
            cur = lax.ppermute(cur, "bus", perm)
        out = lax.dynamic_update_index_in_dim(out, cur, (xi - step * m) % XR, 0)
    return out


def bus_reduce_scatter(flow_part, rider):
    yh, xi, c = bus_place()
    first = [(xi - 1) % XR, (xi + 1) % XR]
    second = [(xi + 2) % XR, xi]
    summed = []
    for group in (first, second):
        send = jnp.stack([flow_part(x, False) for x in group])
        keep = jnp.stack([flow_part(x, True) for x in group])
        summed.append(keep + lax.ppermute(send, "bus", CORE_SWAP))
    a, b = summed
    half = a.shape[2] // 2
    cw, rider = ring_scatter([a[0, :, :half], b[0, :, :half], a[1, :, :half], b[1, :, :half]], True, rider)
    ccw, _ = ring_scatter([a[1, :, half:], b[0, :, half:], a[0, :, half:], b[1, :, half:]], False)
    z = jnp.concatenate([cw, ccw], axis=1)
    return z, rider


def bus_pair_sum(z):
    yh, xi, c = bus_place()
    return pick(z, yh, 0) + lax.ppermute(pick(z, 1 - yh, 0), "bus", Y_SWAP)


def bus_all_gather(p):
    yh, xi, c = bus_place()
    other = lax.ppermute(p, "bus", Y_SWAP)
    pair = jnp.where(yh == 0, jnp.stack([p, other]), jnp.stack([other, p]))
    half = p.shape[0] // 2
    cw = ring_gather(pair[:, :half], xi, True)
    ccw = ring_gather(pair[:, half:], xi, False)
    quad = jnp.moveaxis(jnp.concatenate([cw, ccw], axis=2), 0, 1)
    return quad, lax.ppermute(quad, "bus", CORE_SWAP)


def slots_of(slabs):
    positions = jnp.arange(slabs.shape[-1], dtype=jnp.int32)
    earlier = positions[None, :] < positions[:, None]
    same = slabs[..., :, None] == slabs[..., None, :]
    return jnp.sum((same & earlier).astype(jnp.int32), axis=-1)


def per_device(
    shift_factors,
    injections,
    prices,
    limits,
    unit_cost,
    bus_load,
    bus_capacity,
    irradiance_profile,
    plant_group,
    scenario_profile,
    listed_slab,
    listed_block,
    rent_weight,
):
    scenarios = injections.shape[1]
    bus_axis = lax.axis_size("bus")
    slab_axis = lax.axis_size("br")
    slab_index = lax.axis_index("br")
    column_index = lax.axis_index("bus")
    list_len = listed_slab.shape[1]
    entries = GDEV * list_len
    slab_rows = shift_factors.shape[0]
    blocks_per_slab = slab_rows // BLOCK

    slab_by_device = listed_slab.reshape(-1, entries)
    block_by_device = listed_block.reshape(-1, entries)
    self_device = slab_index * bus_axis + column_index
    own_slab = lax.dynamic_index_in_dim(slab_by_device, self_device, 0, keepdims=False)
    own_slot = slots_of(own_slab)
    slab_range = jnp.arange(slab_axis, dtype=jnp.int32)
    slot_range = jnp.arange(CAP, dtype=jnp.int32)
    pick_out = (own_slab[None, None, :] == slab_range[:, None, None]) & (
        own_slot[None, None, :] == slot_range[None, :, None]
    )
    weight_rows = rent_weight.reshape(entries, BLOCK)
    outgoing_w = jnp.einsum(
        "sce,er->scr", pick_out.astype(jnp.bfloat16), weight_rows, preferred_element_type=jnp.float32
    ).astype(jnp.bfloat16)
    sources = slab_range * bus_axis + column_index
    src_slab = jnp.take(slab_by_device, sources, axis=0)
    src_block = jnp.take(block_by_device, sources, axis=0)
    src_slot = slots_of(src_slab)
    pick_in = (src_slab[:, None, :] == slab_index) & (src_slot[:, None, :] == slot_range[None, :, None])
    block_choice = jnp.sum(jnp.where(pick_in, src_block[:, None, :], 0), axis=2)
    block_hot = block_choice[:, :, None] == jnp.arange(blocks_per_slab, dtype=jnp.int32)[None, None, :]
    yh, xi, core = bus_place()

    bus_rows = injections.shape[0]
    share_rows = bus_rows // slab_axis
    start = slab_index * share_rows
    my_inj = lax.dynamic_slice_in_dim(injections, start, share_rows, 0)
    my_cost = lax.dynamic_slice_in_dim(unit_cost, start, share_rows, 0)
    my_load = lax.dynamic_slice_in_dim(bus_load, start, share_rows, 0)
    my_cap = lax.dynamic_slice_in_dim(bus_capacity, start, share_rows, 0)
    my_group = lax.dynamic_slice_in_dim(plant_group, start, share_rows, 0)
    by_group = jnp.take(irradiance_profile, my_group, axis=1)
    share = jnp.take(by_group, scenario_profile, axis=0).T
    upper = my_cap[:, None] * share
    lower = -my_load[:, None]
    base = my_inj - step_primal * my_cost[:, None]

    inject_half = injections.astype(jnp.bfloat16)
    by_place = shift_factors.reshape(YHI, XR, CORES, -1, shift_factors.shape[1])
    sf_keep = pick(by_place, core, 2)
    sf_send = pick(by_place, 1 - core, 2)

    def flow_part(x, mine):
        rows = pick(sf_keep if mine else sf_send, x, 1)
        return jnp.dot(rows, inject_half, preferred_element_type=jnp.float32)

    ring_out, outgoing_w = bus_reduce_scatter(flow_part, outgoing_w)
    arrived_w = lax.all_to_all(outgoing_w, "br", 0, 0, tiled=True)
    masked = jnp.where(block_hot[:, :, :, None], arrived_w[:, :, None, :], jnp.zeros((), jnp.bfloat16))
    masked = masked.reshape(slab_axis * CAP, YHI, XR, CORES, -1)
    masked_keep = pick(masked, core, 3)
    masked_send = pick(masked, 1 - core, 3)
    ring_out, masked_keep, masked_send, upper, lower, base = lax.optimization_barrier(
        (ring_out, masked_keep, masked_send, upper, lower, base)
    )
    flow = bus_pair_sum(ring_out)
    moved = prices + step_dual * flow
    bound = step_dual * limits[:, None]
    new_prices = moved - jnp.clip(moved, -bound, bound)
    price_half = new_prices.astype(jnp.bfloat16)
    prices_keep, prices_send = bus_all_gather(price_half)
    contract = (((0, 1, 2), (0, 1, 2)), ((), ()))
    partial_grad = lax.dot_general(sf_keep, prices_keep, contract, preferred_element_type=jnp.float32)
    partial_grad = partial_grad + lax.dot_general(sf_send, prices_send, contract, preferred_element_type=jnp.float32)
    contract_w = (((1, 2, 3), (0, 1, 2)), ((), ()))
    partial_rent = lax.dot_general(masked_keep, prices_keep, contract_w, preferred_element_type=jnp.float32)
    partial_rent = partial_rent + lax.dot_general(masked_send, prices_send, contract_w, preferred_element_type=jnp.float32)

    gathered = lax.all_to_all(partial_grad.reshape(slab_axis, share_rows, scenarios), "br", 0, 0, tiled=True)
    gradient = jnp.sum(gathered, axis=0)
    trial = base - step_primal * gradient
    my_new = jnp.minimum(jnp.maximum(trial, lower), upper)
    outgoing = jnp.concatenate(
        [jnp.broadcast_to(my_new[None], (slab_axis, share_rows, scenarios)), partial_rent.reshape(slab_axis, CAP, scenarios)],
        axis=1,
    )
    arrived = lax.all_to_all(outgoing, "br", 0, 0, tiled=True)
    new_injections = arrived[:, :share_rows].reshape(bus_rows, scenarios)
    returned = arrived[:, share_rows:]

    lookup = own_slab * CAP + own_slot
    fetched = jnp.take(returned.reshape(slab_axis * CAP, scenarios), lookup, axis=0)
    group_rent = jnp.sum(fetched.reshape(GDEV, list_len, scenarios), axis=1)
    return (new_injections, new_prices, group_rent)


def solution(mesh):
    placed = (
        P("br", "bus"),
        P("bus", None),
        P(("br", "bus"), None),
        P(("br", "bus")),
        P("bus"),
        P("bus"),
        P("bus"),
        P(),
        P("bus"),
        P(),
        P(),
        P(),
        P(("br", "bus"), None),
    )
    return jax.shard_map(
        per_device,
        mesh=mesh,
        in_specs=placed,
        out_specs=(P("bus", None), P(("br", "bus"), None), P(("br", "bus"), None)),
        check_vma=False,
    )
```
